32 devices in a mesh: sum: 8 (over z, x), mode: 4 (over y, core).
Axes of the slice: x: 2, y: 2, z: 4, core: 2. Of those that a mesh axis runs over, the one named last changes fastest.
Arguments:
- left_cores: bfloat16 [8, 512, 64, 512], P('sum', None, 'mode'), may hold values from -80 to 80, as said below
- right_cores: bfloat16 [8, 512, 64, 512], P('sum', None, 'mode'), may hold values from -6 to 6
- sketch: bfloat16 [64, 512, 512], P('mode'), may hold values from -0.03125 to 0.03125
Outputs:
- basis_core: float32 [512, 64, 512], P('sum', 'mode')
- carries: float32 [8, 512, 512], P('sum')
The draws below stay inside these ranges and needn't reach their ends.
Inputs may be any that keep to these rules, and one draw needn't show every extreme that they name: `left_cores`: independent entries; each row (summand, left rank, mode index) has its own scale.
All inputs are finite; a program needn't handle non-finite values.
Results may differ from the reference program's by a relative error of at most 0.0035.
Values may be sent and summed in bfloat16 or wider, within the bound.
No kernel may reach another device: no remote copies, remote signals or barrier semaphores. Data moves between devices by JAX's collectives and lax.ppermute only.
A program may use at most 128 MiB of HBM per device.

```python
import math
import jax
import jax.numpy as jnp
from jax import lax

R_IN = 512
MODES = 64
RANK = 512
RIGHT = 512
TARGET = 512
SUMMANDS = 8


def draw_left_cores(key, part):
    first, second = jax.random.split(key, 2)
    shape = (SUMMANDS, R_IN, MODES, RANK)
    base = jnp.clip(jax.random.normal(first, shape, jnp.float32), -6.0, 6.0)
    upper = math.log(10.0)
    row_scale = 0.25 * jnp.exp(jax.random.uniform(second, (SUMMANDS, R_IN, MODES, 1), jnp.float32, 0.0, upper))
    rising = 1.0 + 2.0 * jnp.arange(MODES, dtype=jnp.float32) / max(MODES - 1, 1)
    return (base * row_scale * rising.reshape(1, 1, MODES, 1)).astype(jnp.bfloat16)


def shard_levels(rng, shape, shards, least, largest):
    def one(position, parts):
        steps = jax.random.uniform(jax.random.fold_in(jax.random.fold_in(rng, 6), position), (parts,), jnp.float32, least / len(shards), largest / len(shards))
        return jnp.repeat(jnp.exp(steps), shape[position] // parts).reshape((-1,) + (1,) * (len(shape) - position - 1))

    level = one(*shards[0])
    for cut in shards[1:]:
        level = level * one(*cut)
    return level


def normal_values(rng, shape, spread, most, pieces=(), kind=jnp.bfloat16):
    entries = spread * jax.random.normal(rng, shape, jnp.float32)
    if pieces:
        entries = entries * shard_levels(rng, shape, pieces, -0.22, 0.18)
    return jnp.clip(entries, -most, most).astype(kind)


def setup_inputs(seed: int = 0) -> dict:
    streams_of = jax.random.split(jax.random.key(seed), 4)
    return {
        "left_cores": draw_left_cores(jax.random.fold_in(streams_of[3], 71), 0),
        "right_cores": normal_values(streams_of[1], (SUMMANDS, RANK, MODES, RIGHT), 1.0, 6.0, ((0, 8), (2, 4))),
        "sketch": normal_values(streams_of[2], (MODES, RIGHT, TARGET), (MODES * RIGHT) ** -0.5, 0.03125, ((0, 4),)),
    }


def reference(left_cores, right_cores, sketch):
    flat_sketch = sketch.reshape(MODES * RIGHT, TARGET)
    sketched = jnp.zeros((R_IN * MODES, TARGET), jnp.float32)
    for which in range(SUMMANDS):
        mapped = jnp.dot(right_cores[which].reshape(RANK, MODES * RIGHT).astype(jnp.float32), flat_sketch.astype(jnp.float32), preferred_element_type=jnp.float32).astype(jnp.bfloat16)
        sketched = sketched + jnp.dot(left_cores[which].reshape(R_IN * MODES, RANK).astype(jnp.float32), mapped.astype(jnp.float32), preferred_element_type=jnp.float32)
    gram = jnp.dot(sketched.T, sketched, precision=lax.Precision.HIGHEST)
    lower = jnp.linalg.cholesky(gram)
    basis = lax.linalg.triangular_solve(lower, sketched, left_side=False, lower=True, transpose_a=True)
    basis_core = (basis * math.sqrt(R_IN * MODES)).reshape(R_IN, MODES, TARGET)
    rounded = basis.astype(jnp.bfloat16)
    carry_list = []
    for which in range(SUMMANDS):
        carry_list.append(jnp.dot(rounded.T.astype(jnp.float32), left_cores[which].reshape(R_IN * MODES, RANK).astype(jnp.float32), preferred_element_type=jnp.float32))
    return (basis_core, jnp.stack(carry_list))
```

```python
import math

import jax
import jax.numpy as jnp
from jax import lax
from jax.experimental.layout import Layout, with_layout_constraint
from jax.sharding import PartitionSpec as P

R_IN = 512
MODES = 64
BLOCK = 128

HI = lax.Precision.HIGHEST


def mm(a, b):
    return jnp.dot(a, b, precision=HI, preferred_element_type=jnp.float32)


def orthonormal(sketched, gram):
    n = gram.shape[0]
    b = min(BLOCK, n)
    nb = n // b
    eye = jnp.eye(b, dtype=jnp.float32)
    inverses = []
    panels = []
    trailing = gram
    for k in range(nb):
        diag = trailing[:b, :b]
        lkk = jnp.linalg.cholesky(diag)
        ikk = lax.linalg.triangular_solve(lkk, eye, left_side=True, lower=True)
        inverses.append(ikk)
        if k < nb - 1:
            panel = mm(trailing[b:, :b], ikk.T)
            panels.append(panel)
            trailing = trailing[b:, b:] - mm(panel, panel.T)
    blocks = []
    for k in range(nb):
        rhs = sketched[:, k * b:(k + 1) * b]
        if k > 0:
            done = jnp.concatenate(blocks, axis=1)
            lrow = jnp.concatenate(
                [panels[j][(k - j - 1) * b:(k - j) * b] for j in range(k)], axis=1
            )
            rhs = rhs - mm(done, lrow.T)
        blocks.append(mm(rhs, inverses[k].T))
    return jnp.concatenate(blocks, axis=1)


def per_device(left_cores, right_cores, sketch):
    sum_local, rows_in, mode_local, rank_width = left_cores.shape
    target = sketch.shape[2]
    partial_map = lax.dot_general(
        right_cores, sketch, (((2, 3), (0, 1)), ((), ())), preferred_element_type=jnp.float32
    )
    mapped = lax.psum(partial_map, "mode").astype(jnp.bfloat16)
    local_sum = lax.dot_general(
        left_cores, mapped, (((0, 3), (0, 1)), ((), ())), preferred_element_type=jnp.float32
    )
    local_sum = with_layout_constraint(local_sum, Layout(major_to_minor=(0, 1, 2)))
    factor = math.sqrt(R_IN * MODES)
    share = lax.psum_scatter(local_sum, "sum", scatter_dimension=0, tiled=True)
    flat_share = share.reshape(-1, target)
    gram_part = jnp.dot(flat_share.T, flat_share, precision=HI)
    gram = lax.psum(gram_part, ("sum", "mode"))
    basis = orthonormal(flat_share, gram)
    block = basis.reshape(share.shape)
    rounded = block.astype(jnp.bfloat16)
    pieces = lax.all_gather(rounded, "sum", axis=0, tiled=True)
    partial_carry = lax.dot_general(
        pieces, left_cores, (((0, 1), (1, 2)), ((), ())), preferred_element_type=jnp.float32
    )
    partial_carry = jnp.transpose(partial_carry, (1, 0, 2))
    carries = lax.psum(partial_carry, "mode")
    return (block * factor, carries)


def solution(mesh):
    in_specs = (P("sum", None, "mode", None), P("sum", None, "mode", None), P("mode", None, None))
    out_specs = (P("sum", "mode", None), P("sum", None, None))
    return jax.shard_map(
        per_device, mesh=mesh, in_specs=in_specs, out_specs=out_specs, check_vma=False
    )
```

```python
import math

import jax
import jax.numpy as jnp
from jax import lax
from jax.experimental.layout import Layout, with_layout_constraint
from jax.sharding import PartitionSpec as P

R_IN = 512
MODES = 64
BLOCK = 128

HI = lax.Precision.HIGHEST


def mm(a, b):
    return jnp.dot(a, b, precision=HI, preferred_element_type=jnp.float32)


def orthonormal(sketched, gram):
    n = gram.shape[0]
    b = min(BLOCK, n)
    nb = n // b
    eye = jnp.eye(b, dtype=jnp.float32)
    inverses = []
    panels = []
    trailing = gram
    for k in range(nb):
        diag = trailing[:b, :b]
        lkk = jnp.linalg.cholesky(diag)
        ikk = lax.linalg.triangular_solve(lkk, eye, left_side=True, lower=True)
        inverses.append(ikk)
        if k < nb - 1:
            panel = mm(trailing[b:, :b], ikk.T)
            panels.append(panel)
            trailing = trailing[b:, b:] - mm(panel, panel.T)
    blocks = []
    for k in range(nb):
        rhs = sketched[:, k * b:(k + 1) * b]
        if k > 0:
            done = jnp.concatenate(blocks, axis=1)
            lrow = jnp.concatenate(
                [panels[j][(k - j - 1) * b:(k - j) * b] for j in range(k)], axis=1
            )
            rhs = rhs - mm(done, lrow.T)
        blocks.append(mm(rhs, inverses[k].T))
    return jnp.concatenate(blocks, axis=1)


def per_device(left_cores, right_cores, sketch):
    sum_local, rows_in, mode_local, rank_width = left_cores.shape
    target = sketch.shape[2]
    partial_map = lax.dot_general(
        right_cores, sketch, (((2, 3), (0, 1)), ((), ())), preferred_element_type=jnp.float32
    )
    mapped = lax.psum(partial_map, "mode").astype(jnp.bfloat16)
    local_sum = lax.dot_general(
        left_cores, mapped, (((0, 3), (0, 1)), ((), ())), preferred_element_type=jnp.float32
    )
    local_sum = with_layout_constraint(local_sum, Layout(major_to_minor=(0, 1, 2)))
    factor = math.sqrt(R_IN * MODES)
    share = lax.psum_scatter(local_sum, "sum", scatter_dimension=0, tiled=True)
    flat_share = share.reshape(-1, target)
    gram_part = jnp.dot(flat_share.T, flat_share, precision=HI)
    gram = lax.psum(lax.psum(gram_part, "mode"), "sum")
    basis = orthonormal(flat_share, gram)
    block = basis.reshape(share.shape)
    rounded = block.astype(jnp.bfloat16)
    pieces = lax.all_gather(rounded, "sum", axis=0, tiled=True)
    partial_carry = lax.dot_general(
        pieces, left_cores, (((0, 1), (1, 2)), ((), ())), preferred_element_type=jnp.float32
    )
    partial_carry = jnp.transpose(partial_carry, (1, 0, 2))
    carries = lax.psum(partial_carry, "mode")
    return (block * factor, carries)


def solution(mesh):
    in_specs = (P("sum", None, "mode", None), P("sum", None, "mode", None), P("mode", None, None))
    out_specs = (P("sum", "mode", None), P("sum", None, None))
    return jax.shard_map(
        per_device, mesh=mesh, in_specs=in_specs, out_specs=out_specs, check_vma=False
    )
```

```python
import functools
import math

import jax
import jax.numpy as jnp
from jax import lax
from jax.experimental.layout import Layout, with_layout_constraint
from jax.sharding import PartitionSpec as P

R_IN = 512
MODES = 64
BLOCK = 128

HI = lax.Precision.HIGHEST


def mm(a, b):
    return jnp.dot(a, b, precision=HI, preferred_element_type=jnp.float32)


def orthonormal(sketched, gram):
    n = gram.shape[0]
    b = min(BLOCK, n)
    nb = n // b
    eye = jnp.eye(b, dtype=jnp.float32)
    inverses = []
    panels = []
    trailing = gram
    for k in range(nb):
        diag = trailing[:b, :b]
        lkk = jnp.linalg.cholesky(diag)
        ikk = lax.linalg.triangular_solve(lkk, eye, left_side=True, lower=True)
        inverses.append(ikk)
        if k < nb - 1:
            panel = mm(trailing[b:, :b], ikk.T)
            panels.append(panel)
            trailing = trailing[b:, b:] - mm(panel, panel.T)
    blocks = []
    for k in range(nb):
        rhs = sketched[:, k * b:(k + 1) * b]
        if k > 0:
            done = jnp.concatenate(blocks, axis=1)
            lrow = jnp.concatenate(
                [panels[j][(k - j - 1) * b:(k - j) * b] for j in range(k)], axis=1
            )
            rhs = rhs - mm(done, lrow.T)
        blocks.append(mm(rhs, inverses[k].T))
    return jnp.concatenate(blocks, axis=1)


def ring_order(mesh):
    n = mesh.shape["sum"]
    plain = list(range(n))
    try:
        coords = [tuple(int(c) for c in mesh.devices[i, 0].coords) for i in range(n)]
    except (AttributeError, TypeError, IndexError):
        return plain
    axes = [d for d in range(len(coords[0])) if len({c[d] for c in coords}) > 1]
    if len(axes) != 2:
        return plain
    values = [sorted({c[d] for c in coords}) for d in axes]
    if len(values[0]) % 2:
        axes, values = axes[::-1], values[::-1]
    if len(values[0]) % 2 or len(values[0]) * len(values[1]) != n:
        return plain
    where = {(c[axes[0]], c[axes[1]]): i for i, c in enumerate(coords)}
    first, second = values
    cells = [(a, second[0]) for a in first]
    for row, a in enumerate(reversed(first)):
        cols = second[1:] if row % 2 == 0 else second[1:][::-1]
        cells.extend((a, b) for b in cols)
    if len(set(cells)) != n or any(cell not in where for cell in cells):
        return plain
    return [where[cell] for cell in cells]


def ring_reduce_scatter(local, ring):
    n = len(ring)
    rows = local.shape[0] // n
    half = rows // 2
    pos = [0] * n
    for p, i in enumerate(ring):
        pos[i] = p
    me = lax.axis_index("sum")
    fwd = [(ring[p], ring[(p + 1) % n]) for p in range(n)]
    bwd = [(ring[p], ring[(p - 1) % n]) for p in range(n)]

    def table(shift, sign):
        return jnp.asarray(
            [[ring[(pos[i] + sign * (shift + t)) % n] for i in range(n)] for t in range(n)],
            dtype=jnp.int32,
        )

    fwd_blocks = table(1, -1)
    bwd_blocks = table(1, 1)

    def piece(block, offset, size):
        start = block * rows + offset
        return lax.dynamic_slice_in_dim(local, start, size, axis=0)

    acc_f = piece(fwd_blocks[0, me], 0, half)
    acc_b = piece(bwd_blocks[0, me], half, rows - half)
    for t in range(1, n):
        acc_f = lax.ppermute(acc_f, "sum", fwd) + piece(fwd_blocks[t, me], 0, half)
        acc_b = lax.ppermute(acc_b, "sum", bwd) + piece(bwd_blocks[t, me], half, rows - half)
    return jnp.concatenate([acc_f, acc_b], axis=0)


def per_device(ring, left_cores, right_cores, sketch):
    sum_local, rows_in, mode_local, rank_width = left_cores.shape
    target = sketch.shape[2]
    partial_map = lax.dot_general(
        right_cores, sketch, (((2, 3), (0, 1)), ((), ())), preferred_element_type=jnp.float32
    )
    mapped = lax.psum(partial_map, "mode").astype(jnp.bfloat16)
    local_sum = lax.dot_general(
        left_cores, mapped, (((0, 3), (0, 1)), ((), ())), preferred_element_type=jnp.float32
    )
    local_sum = with_layout_constraint(local_sum, Layout(major_to_minor=(0, 1, 2)))
    factor = math.sqrt(R_IN * MODES)
    share = ring_reduce_scatter(local_sum, ring)
    flat_share = share.reshape(-1, target)
    gram_part = jnp.dot(flat_share.T, flat_share, precision=HI)
    gram = lax.psum(lax.psum(gram_part, "mode"), "sum")
    basis = orthonormal(flat_share, gram)
    block = basis.reshape(share.shape)
    rounded = block.astype(jnp.bfloat16)
    pieces = lax.all_gather(rounded, "sum", axis=0, tiled=True)
    partial_carry = lax.dot_general(
        pieces, left_cores, (((0, 1), (1, 2)), ((), ())), preferred_element_type=jnp.float32
    )
    partial_carry = jnp.transpose(partial_carry, (1, 0, 2))
    carries = lax.psum(partial_carry, "mode")
    return (block * factor, carries)


def solution(mesh):
    in_specs = (P("sum", None, "mode", None), P("sum", None, "mode", None), P("mode", None, None))
    out_specs = (P("sum", "mode", None), P("sum", None, None))
    ring = ring_order(mesh)
    return jax.shard_map(
        functools.partial(per_device, ring), mesh=mesh, in_specs=in_specs, out_specs=out_specs, check_vma=False
    )
```

```python
import functools
import math

import jax
import jax.numpy as jnp
from jax import lax
from jax.experimental.layout import Layout, with_layout_constraint
from jax.sharding import PartitionSpec as P

R_IN = 512
MODES = 64
BLOCK = 128

HI = lax.Precision.HIGHEST


def mm(a, b):
    return jnp.dot(a, b, precision=HI, preferred_element_type=jnp.float32)


def orthonormal(sketched, gram):
    n = gram.shape[0]
    b = min(BLOCK, n)
    nb = n // b
    eye = jnp.eye(b, dtype=jnp.float32)
    inverses = []
    panels = []
    trailing = gram
    for k in range(nb):
        diag = trailing[:b, :b]
        lkk = jnp.linalg.cholesky(diag)
        ikk = lax.linalg.triangular_solve(lkk, eye, left_side=True, lower=True)
        inverses.append(ikk)
        if k < nb - 1:
            panel = mm(trailing[b:, :b], ikk.T)
            panels.append(panel)
            trailing = trailing[b:, b:] - mm(panel, panel.T)
    blocks = []
    for k in range(nb):
        rhs = sketched[:, k * b:(k + 1) * b]
        if k > 0:
            done = jnp.concatenate(blocks, axis=1)
            lrow = jnp.concatenate(
                [panels[j][(k - j - 1) * b:(k - j) * b] for j in range(k)], axis=1
            )
            rhs = rhs - mm(done, lrow.T)
        blocks.append(mm(rhs, inverses[k].T))
    return jnp.concatenate(blocks, axis=1)


def ring_order(mesh):
    n = mesh.shape["sum"]
    plain = list(range(n))
    try:
        coords = [tuple(int(c) for c in mesh.devices[i, 0].coords) for i in range(n)]
    except (AttributeError, TypeError, IndexError):
        return plain
    axes = [d for d in range(len(coords[0])) if len({c[d] for c in coords}) > 1]
    if len(axes) != 2:
        return plain
    values = [sorted({c[d] for c in coords}) for d in axes]
    if len(values[0]) % 2:
        axes, values = axes[::-1], values[::-1]
    if len(values[0]) % 2 or len(values[0]) * len(values[1]) != n:
        return plain
    where = {(c[axes[0]], c[axes[1]]): i for i, c in enumerate(coords)}
    first, second = values
    cells = [(a, second[0]) for a in first]
    for row, a in enumerate(reversed(first)):
        cols = second[1:] if row % 2 == 0 else second[1:][::-1]
        cells.extend((a, b) for b in cols)
    if len(set(cells)) != n or any(cell not in where for cell in cells):
        return plain
    return [where[cell] for cell in cells]


def ring_reduce_scatter(local, ring):
    n = len(ring)
    rows = local.shape[0] // n
    half = rows // 2
    pos = [0] * n
    for p, i in enumerate(ring):
        pos[i] = p
    me = lax.axis_index("sum")
    fwd = [(ring[p], ring[(p + 1) % n]) for p in range(n)]
    bwd = [(ring[p], ring[(p - 1) % n]) for p in range(n)]

    def table(shift, sign):
        return jnp.asarray(
            [[ring[(pos[i] + sign * (shift + t)) % n] for i in range(n)] for t in range(n)],
            dtype=jnp.int32,
        )

    fwd_blocks = table(1, -1)
    bwd_blocks = table(1, 1)

    def piece(block, offset, size):
        start = block * rows + offset
        return lax.dynamic_slice_in_dim(local, start, size, axis=0)

    acc_f = piece(fwd_blocks[0, me], 0, half)
    acc_b = piece(bwd_blocks[0, me], half, rows - half)
    for t in range(1, n):
        acc_f = lax.ppermute(acc_f, "sum", fwd) + piece(fwd_blocks[t, me], 0, half)
        acc_b = lax.ppermute(acc_b, "sum", bwd) + piece(bwd_blocks[t, me], half, rows - half)
    return jnp.concatenate([acc_f, acc_b], axis=0)


def ring_gather_carries(own, left_cores, ring):
    n = len(ring)
    rows = own.shape[0]
    half = rows // 2
    pos = [0] * n
    for p, i in enumerate(ring):
        pos[i] = p
    me = lax.axis_index("sum")
    fwd = [(ring[p], ring[(p + 1) % n]) for p in range(n)]
    bwd = [(ring[p], ring[(p - 1) % n]) for p in range(n)]
    fwd_blocks = jnp.asarray(
        [[ring[(pos[i] - t) % n] for i in range(n)] for t in range(n)], dtype=jnp.int32
    )
    bwd_blocks = jnp.asarray(
        [[ring[(pos[i] + t) % n] for i in range(n)] for t in range(n)], dtype=jnp.int32
    )

    def term(piece, block, offset):
        start = block * rows + offset
        lhs = lax.dynamic_slice_in_dim(left_cores, start, piece.shape[0], axis=1)
        return lax.dot_general(
            piece, lhs, (((0, 1), (1, 2)), ((), ())), preferred_element_type=jnp.float32
        )

    hold_f = own[:half]
    hold_b = own[half:]
    total = term(hold_f, fwd_blocks[0, me], 0) + term(hold_b, bwd_blocks[0, me], half)
    for t in range(1, n):
        hold_f = lax.ppermute(hold_f, "sum", fwd)
        hold_b = lax.ppermute(hold_b, "sum", bwd)
        total = total + term(hold_f, fwd_blocks[t, me], 0)
        total = total + term(hold_b, bwd_blocks[t, me], half)
    return jnp.transpose(total, (1, 0, 2))


def per_device(ring, left_cores, right_cores, sketch):
    sum_local, rows_in, mode_local, rank_width = left_cores.shape
    target = sketch.shape[2]
    partial_map = lax.dot_general(
        right_cores, sketch, (((2, 3), (0, 1)), ((), ())), preferred_element_type=jnp.float32
    )
    mapped = lax.psum(partial_map, "mode").astype(jnp.bfloat16)
    local_sum = lax.dot_general(
        left_cores, mapped, (((0, 3), (0, 1)), ((), ())), preferred_element_type=jnp.float32
    )
    local_sum = with_layout_constraint(local_sum, Layout(major_to_minor=(0, 1, 2)))
    factor = math.sqrt(R_IN * MODES)
    share = ring_reduce_scatter(local_sum, ring)
    flat_share = share.reshape(-1, target)
    gram_part = jnp.dot(flat_share.T, flat_share, precision=HI)
    gram = lax.psum(lax.psum(gram_part, "mode"), "sum")
    basis = orthonormal(flat_share, gram)
    block = basis.reshape(share.shape)
    rounded = block.astype(jnp.bfloat16)
    partial_carry = ring_gather_carries(rounded, left_cores, ring)
    carries = lax.psum(partial_carry, "mode")
    return (block * factor, carries)


def solution(mesh):
    in_specs = (P("sum", None, "mode", None), P("sum", None, "mode", None), P("mode", None, None))
    out_specs = (P("sum", "mode", None), P("sum", None, None))
    ring = ring_order(mesh)
    return jax.shard_map(
        functools.partial(per_device, ring), mesh=mesh, in_specs=in_specs, out_specs=out_specs, check_vma=False
    )
```

```python
import functools
import math

import jax
import jax.numpy as jnp
from jax import lax
from jax.experimental.layout import Layout, with_layout_constraint
from jax.sharding import PartitionSpec as P

R_IN = 512
MODES = 64
BLOCK = 128

HI = lax.Precision.HIGHEST


def mm(a, b):
    return jnp.dot(a, b, precision=HI, preferred_element_type=jnp.float32)


def orthonormal(sketched, gram):
    n = gram.shape[0]
    b = min(BLOCK, n)
    nb = n // b
    eye = jnp.eye(b, dtype=jnp.float32)
    inverses = []
    panels = []
    trailing = gram
    for k in range(nb):
        diag = trailing[:b, :b]
        lkk = jnp.linalg.cholesky(diag)
        ikk = lax.linalg.triangular_solve(lkk, eye, left_side=True, lower=True)
        inverses.append(ikk)
        if k < nb - 1:
            panel = mm(trailing[b:, :b], ikk.T)
            panels.append(panel)
            trailing = trailing[b:, b:] - mm(panel, panel.T)
    blocks = []
    for k in range(nb):
        rhs = sketched[:, k * b:(k + 1) * b]
        if k > 0:
            done = jnp.concatenate(blocks, axis=1)
            lrow = jnp.concatenate(
                [panels[j][(k - j - 1) * b:(k - j) * b] for j in range(k)], axis=1
            )
            rhs = rhs - mm(done, lrow.T)
        blocks.append(mm(rhs, inverses[k].T))
    return jnp.concatenate(blocks, axis=1)


def ring_order(mesh):
    n = mesh.shape["sum"]
    plain = list(range(n))
    try:
        coords = [tuple(int(c) for c in mesh.devices[i, 0].coords) for i in range(n)]
    except (AttributeError, TypeError, IndexError):
        return plain
    axes = [d for d in range(len(coords[0])) if len({c[d] for c in coords}) > 1]
    if len(axes) != 2:
        return plain
    values = [sorted({c[d] for c in coords}) for d in axes]
    if len(values[0]) % 2:
        axes, values = axes[::-1], values[::-1]
    if len(values[0]) % 2 or len(values[0]) * len(values[1]) != n:
        return plain
    where = {(c[axes[0]], c[axes[1]]): i for i, c in enumerate(coords)}
    first, second = values
    cells = [(a, second[0]) for a in first]
    for row, a in enumerate(reversed(first)):
        cols = second[1:] if row % 2 == 0 else second[1:][::-1]
        cells.extend((a, b) for b in cols)
    if len(set(cells)) != n or any(cell not in where for cell in cells):
        return plain
    return [where[cell] for cell in cells]


def ring_reduce_scatter(local, ring):
    n = len(ring)
    rows = local.shape[0] // n
    half = rows // 2
    pos = [0] * n
    for p, i in enumerate(ring):
        pos[i] = p
    me = lax.axis_index("sum")
    fwd = [(ring[p], ring[(p + 1) % n]) for p in range(n)]
    bwd = [(ring[p], ring[(p - 1) % n]) for p in range(n)]

    def table(shift, sign):
        return jnp.asarray(
            [[ring[(pos[i] + sign * (shift + t)) % n] for i in range(n)] for t in range(n)],
            dtype=jnp.int32,
        )

    fwd_blocks = table(1, -1)
    bwd_blocks = table(1, 1)

    def piece(block, offset, size):
        start = block * rows + offset
        return lax.dynamic_slice_in_dim(local, start, size, axis=0)

    acc_f = piece(fwd_blocks[0, me], 0, half)
    acc_b = piece(bwd_blocks[0, me], half, rows - half)
    for t in range(1, n):
        acc_f = lax.ppermute(acc_f, "sum", fwd) + piece(fwd_blocks[t, me], 0, half)
        acc_b = lax.ppermute(acc_b, "sum", bwd) + piece(bwd_blocks[t, me], half, rows - half)
    return jnp.concatenate([acc_f, acc_b], axis=0)


def ring_gather_carries(own, left_cores, ring):
    n = len(ring)
    rows = own.shape[0]
    half = rows // 2
    pos = [0] * n
    for p, i in enumerate(ring):
        pos[i] = p
    me = lax.axis_index("sum")
    fwd = [(ring[p], ring[(p + 1) % n]) for p in range(n)]
    bwd = [(ring[p], ring[(p - 1) % n]) for p in range(n)]
    fwd_blocks = jnp.asarray(
        [[ring[(pos[i] - t) % n] for i in range(n)] for t in range(n)], dtype=jnp.int32
    )
    bwd_blocks = jnp.asarray(
        [[ring[(pos[i] + t) % n] for i in range(n)] for t in range(n)], dtype=jnp.int32
    )

    def term(piece, block, offset):
        start = block * rows + offset
        lhs = lax.dynamic_slice_in_dim(left_cores, start, piece.shape[0], axis=1)
        return lax.dot_general(
            piece, lhs, (((0, 1), (1, 2)), ((), ())), preferred_element_type=jnp.float32
        )

    hold_f = own[:half]
    hold_b = own[half:]
    total = term(hold_f, fwd_blocks[0, me], 0) + term(hold_b, bwd_blocks[0, me], half)
    for t in range(1, n):
        hold_f = lax.ppermute(hold_f, "sum", fwd)
        hold_b = lax.ppermute(hold_b, "sum", bwd)
        total = total + term(hold_f, fwd_blocks[t, me], 0)
        total = total + term(hold_b, bwd_blocks[t, me], half)
    return jnp.transpose(total, (1, 0, 2))


def ring_all_gather(own, ring):
    n = len(ring)
    rows = own.shape[0]
    half = rows // 2
    pos = [0] * n
    for p, i in enumerate(ring):
        pos[i] = p
    me = lax.axis_index("sum")
    fwd = [(ring[p], ring[(p + 1) % n]) for p in range(n)]
    bwd = [(ring[p], ring[(p - 1) % n]) for p in range(n)]
    fwd_blocks = jnp.asarray(
        [[ring[(pos[i] - t) % n] for i in range(n)] for t in range(n)], dtype=jnp.int32
    )
    bwd_blocks = jnp.asarray(
        [[ring[(pos[i] + t) % n] for i in range(n)] for t in range(n)], dtype=jnp.int32
    )
    out = jnp.zeros((n * rows,) + own.shape[1:], own.dtype)
    hold_f = own[:half]
    hold_b = own[half:]
    for t in range(n):
        if t:
            hold_f = lax.ppermute(hold_f, "sum", fwd)
            hold_b = lax.ppermute(hold_b, "sum", bwd)
        out = lax.dynamic_update_slice_in_dim(out, hold_f, fwd_blocks[t, me] * rows, axis=0)
        out = lax.dynamic_update_slice_in_dim(
            out, hold_b, bwd_blocks[t, me] * rows + half, axis=0
        )
    return out


def per_device(ring, left_cores, right_cores, sketch):
    sum_local, rows_in, mode_local, rank_width = left_cores.shape
    target = sketch.shape[2]
    partial_map = lax.dot_general(
        right_cores, sketch, (((2, 3), (0, 1)), ((), ())), preferred_element_type=jnp.float32
    )
    mapped = lax.psum(partial_map, "mode").astype(jnp.bfloat16)
    local_sum = lax.dot_general(
        left_cores, mapped, (((0, 3), (0, 1)), ((), ())), preferred_element_type=jnp.float32
    )
    local_sum = with_layout_constraint(local_sum, Layout(major_to_minor=(0, 1, 2)))
    factor = math.sqrt(R_IN * MODES)
    share = ring_reduce_scatter(local_sum, ring)
    flat_share = share.reshape(-1, target)
    gram_part = jnp.dot(flat_share.T, flat_share, precision=HI)
    gram_mode = lax.psum(gram_part, "mode")
    gram = ring_all_gather(ring_reduce_scatter(gram_mode, ring), ring)
    basis = orthonormal(flat_share, gram)
    block = basis.reshape(share.shape)
    rounded = block.astype(jnp.bfloat16)
    partial_carry = ring_gather_carries(rounded, left_cores, ring)
    carries = lax.psum(partial_carry, "mode")
    return (block * factor, carries)


def solution(mesh):
    in_specs = (P("sum", None, "mode", None), P("sum", None, "mode", None), P("mode", None, None))
    out_specs = (P("sum", "mode", None), P("sum", None, None))
    ring = ring_order(mesh)
    return jax.shard_map(
        functools.partial(per_device, ring), mesh=mesh, in_specs=in_specs, out_specs=out_specs, check_vma=False
    )
```

```python
import functools
import math

import jax
import jax.numpy as jnp
from jax import lax
from jax.experimental.layout import Layout, with_layout_constraint
from jax.sharding import PartitionSpec as P

R_IN = 512
MODES = 64
BLOCK = 128

HI = lax.Precision.HIGHEST


def mm(a, b):
    return jnp.dot(a, b, precision=HI, preferred_element_type=jnp.float32)


def orthonormal(sketched, gram):
    n = gram.shape[0]
    b = min(BLOCK, n)
    nb = n // b
    eye = jnp.eye(b, dtype=jnp.float32)
    inverses = []
    panels = []
    trailing = gram
    for k in range(nb):
        diag = trailing[:b, :b]
        lkk = jnp.linalg.cholesky(diag)
        ikk = lax.linalg.triangular_solve(lkk, eye, left_side=True, lower=True)
        inverses.append(ikk)
        if k < nb - 1:
            panel = mm(trailing[b:, :b], ikk.T)
            panels.append(panel)
            trailing = trailing[b:, b:] - mm(panel, panel.T)
    blocks = []
    for k in range(nb):
        rhs = sketched[:, k * b:(k + 1) * b]
        if k > 0:
            done = jnp.concatenate(blocks, axis=1)
            lrow = jnp.concatenate(
                [panels[j][(k - j - 1) * b:(k - j) * b] for j in range(k)], axis=1
            )
            rhs = rhs - mm(done, lrow.T)
        blocks.append(mm(rhs, inverses[k].T))
    return jnp.concatenate(blocks, axis=1)


def symmetric_psum(gram_part):
    n = gram_part.shape[0]
    b = min(BLOCK, n)
    nb = n // b
    lower = [(i, j) for i in range(nb) for j in range(i + 1)]
    packed = jnp.stack([gram_part[i * b:(i + 1) * b, j * b:(j + 1) * b] for i, j in lower])
    packed = lax.psum(lax.psum(packed, "mode"), "sum")
    where = {cell: k for k, cell in enumerate(lower)}
    rows = []
    for i in range(nb):
        row = []
        for j in range(nb):
            row.append(packed[where[(i, j)]] if j <= i else packed[where[(j, i)]].T)
        rows.append(jnp.concatenate(row, axis=1))
    return jnp.concatenate(rows, axis=0)


def ring_order(mesh):
    n = mesh.shape["sum"]
    plain = list(range(n))
    try:
        coords = [tuple(int(c) for c in mesh.devices[i, 0].coords) for i in range(n)]
    except (AttributeError, TypeError, IndexError):
        return plain
    axes = [d for d in range(len(coords[0])) if len({c[d] for c in coords}) > 1]
    if len(axes) != 2:
        return plain
    values = [sorted({c[d] for c in coords}) for d in axes]
    if len(values[0]) % 2:
        axes, values = axes[::-1], values[::-1]
    if len(values[0]) % 2 or len(values[0]) * len(values[1]) != n:
        return plain
    where = {(c[axes[0]], c[axes[1]]): i for i, c in enumerate(coords)}
    first, second = values
    cells = [(a, second[0]) for a in first]
    for row, a in enumerate(reversed(first)):
        cols = second[1:] if row % 2 == 0 else second[1:][::-1]
        cells.extend((a, b) for b in cols)
    if len(set(cells)) != n or any(cell not in where for cell in cells):
        return plain
    return [where[cell] for cell in cells]


def ring_reduce_scatter(local, ring):
    n = len(ring)
    rows = local.shape[0] // n
    half = rows // 2
    pos = [0] * n
    for p, i in enumerate(ring):
        pos[i] = p
    me = lax.axis_index("sum")
    fwd = [(ring[p], ring[(p + 1) % n]) for p in range(n)]
    bwd = [(ring[p], ring[(p - 1) % n]) for p in range(n)]

    def table(shift, sign):
        return jnp.asarray(
            [[ring[(pos[i] + sign * (shift + t)) % n] for i in range(n)] for t in range(n)],
            dtype=jnp.int32,
        )

    fwd_blocks = table(1, -1)
    bwd_blocks = table(1, 1)

    def piece(block, offset, size):
        start = block * rows + offset
        return lax.dynamic_slice_in_dim(local, start, size, axis=0)

    acc_f = piece(fwd_blocks[0, me], 0, half)
    acc_b = piece(bwd_blocks[0, me], half, rows - half)
    for t in range(1, n):
        acc_f = lax.ppermute(acc_f, "sum", fwd) + piece(fwd_blocks[t, me], 0, half)
        acc_b = lax.ppermute(acc_b, "sum", bwd) + piece(bwd_blocks[t, me], half, rows - half)
    return jnp.concatenate([acc_f, acc_b], axis=0)


def ring_gather_carries(own, left_cores, ring):
    n = len(ring)
    rows = own.shape[0]
    half = rows // 2
    pos = [0] * n
    for p, i in enumerate(ring):
        pos[i] = p
    me = lax.axis_index("sum")
    fwd = [(ring[p], ring[(p + 1) % n]) for p in range(n)]
    bwd = [(ring[p], ring[(p - 1) % n]) for p in range(n)]
    fwd_blocks = jnp.asarray(
        [[ring[(pos[i] - t) % n] for i in range(n)] for t in range(n)], dtype=jnp.int32
    )
    bwd_blocks = jnp.asarray(
        [[ring[(pos[i] + t) % n] for i in range(n)] for t in range(n)], dtype=jnp.int32
    )

    def term(piece, block, offset):
        start = block * rows + offset
        lhs = lax.dynamic_slice_in_dim(left_cores, start, piece.shape[0], axis=1)
        return lax.dot_general(
            piece, lhs, (((0, 1), (1, 2)), ((), ())), preferred_element_type=jnp.float32
        )

    hold_f = own[:half]
    hold_b = own[half:]
    total = term(hold_f, fwd_blocks[0, me], 0) + term(hold_b, bwd_blocks[0, me], half)
    for t in range(1, n):
        hold_f = lax.ppermute(hold_f, "sum", fwd)
        hold_b = lax.ppermute(hold_b, "sum", bwd)
        total = total + term(hold_f, fwd_blocks[t, me], 0)
        total = total + term(hold_b, bwd_blocks[t, me], half)
    return jnp.transpose(total, (1, 0, 2))


def per_device(ring, left_cores, right_cores, sketch):
    sum_local, rows_in, mode_local, rank_width = left_cores.shape
    target = sketch.shape[2]
    partial_map = lax.dot_general(
        right_cores, sketch, (((2, 3), (0, 1)), ((), ())), preferred_element_type=jnp.float32
    )
    mapped = lax.psum(partial_map, "mode").astype(jnp.bfloat16)
    local_sum = lax.dot_general(
        left_cores, mapped, (((0, 3), (0, 1)), ((), ())), preferred_element_type=jnp.float32
    )
    local_sum = with_layout_constraint(local_sum, Layout(major_to_minor=(0, 1, 2)))
    factor = math.sqrt(R_IN * MODES)
    share = ring_reduce_scatter(local_sum, ring)
    flat_share = share.reshape(-1, target)
    gram_part = jnp.dot(flat_share.T, flat_share, precision=HI)
    gram = symmetric_psum(gram_part)
    basis = orthonormal(flat_share, gram)
    block = basis.reshape(share.shape)
    rounded = block.astype(jnp.bfloat16)
    partial_carry = ring_gather_carries(rounded, left_cores, ring)
    carries = lax.psum(partial_carry, "mode")
    return (block * factor, carries)


def solution(mesh):
    in_specs = (P("sum", None, "mode", None), P("sum", None, "mode", None), P("mode", None, None))
    out_specs = (P("sum", "mode", None), P("sum", None, None))
    ring = ring_order(mesh)
    return jax.shard_map(
        functools.partial(per_device, ring), mesh=mesh, in_specs=in_specs, out_specs=out_specs, check_vma=False
    )
```

```python
import functools
import math

import jax
import jax.numpy as jnp
from jax import lax
from jax.experimental.layout import Layout, with_layout_constraint
from jax.sharding import PartitionSpec as P

R_IN = 512
MODES = 64
BLOCK = 128

HI = lax.Precision.HIGHEST


def mm(a, b):
    return jnp.dot(a, b, precision=HI, preferred_element_type=jnp.float32)


def orthonormal(sketched, gram):
    n = gram.shape[0]
    b = min(BLOCK, n)
    nb = n // b
    eye = jnp.eye(b, dtype=jnp.float32)
    inverses = []
    panels = []
    trailing = gram
    for k in range(nb):
        diag = trailing[:b, :b]
        lkk = jnp.linalg.cholesky(diag)
        ikk = lax.linalg.triangular_solve(lkk, eye, left_side=True, lower=True)
        inverses.append(ikk)
        if k < nb - 1:
            panel = mm(trailing[b:, :b], ikk.T)
            panels.append(panel)
            trailing = trailing[b:, b:] - mm(panel, panel.T)
    blocks = []
    for k in range(nb):
        rhs = sketched[:, k * b:(k + 1) * b]
        if k > 0:
            done = jnp.concatenate(blocks, axis=1)
            lrow = jnp.concatenate(
                [panels[j][(k - j - 1) * b:(k - j) * b] for j in range(k)], axis=1
            )
            rhs = rhs - mm(done, lrow.T)
        blocks.append(mm(rhs, inverses[k].T))
    return jnp.concatenate(blocks, axis=1)


def symmetric_psum(gram_part):
    n = gram_part.shape[0]
    b = min(BLOCK, n)
    nb = n // b
    lower = [(i, j) for i in range(nb) for j in range(i + 1)]
    packed = jnp.stack([gram_part[i * b:(i + 1) * b, j * b:(j + 1) * b] for i, j in lower])
    packed = lax.psum(lax.psum(packed, "mode"), "sum")
    where = {cell: k for k, cell in enumerate(lower)}
    rows = []
    for i in range(nb):
        row = []
        for j in range(nb):
            row.append(packed[where[(i, j)]] if j <= i else packed[where[(j, i)]].T)
        rows.append(jnp.concatenate(row, axis=1))
    return jnp.concatenate(rows, axis=0)


def ring_order(mesh):
    n = mesh.shape["sum"]
    plain = list(range(n))
    try:
        coords = [tuple(int(c) for c in mesh.devices[i, 0].coords) for i in range(n)]
    except (AttributeError, TypeError, IndexError):
        return plain
    axes = [d for d in range(len(coords[0])) if len({c[d] for c in coords}) > 1]
    if len(axes) != 2:
        return plain
    values = [sorted({c[d] for c in coords}) for d in axes]
    if len(values[0]) % 2:
        axes, values = axes[::-1], values[::-1]
    if len(values[0]) % 2 or len(values[0]) * len(values[1]) != n:
        return plain
    where = {(c[axes[0]], c[axes[1]]): i for i, c in enumerate(coords)}
    first, second = values
    cells = [(a, second[0]) for a in first]
    for row, a in enumerate(reversed(first)):
        cols = second[1:] if row % 2 == 0 else second[1:][::-1]
        cells.extend((a, b) for b in cols)
    if len(set(cells)) != n or any(cell not in where for cell in cells):
        return plain
    return [where[cell] for cell in cells]


def ring_reduce_scatter(local, total_rows, ring):
    n = len(ring)
    rows = total_rows // n
    half = rows // 2
    pos = [0] * n
    for p, i in enumerate(ring):
        pos[i] = p
    me = lax.axis_index("sum")
    fwd = [(ring[p], ring[(p + 1) % n]) for p in range(n)]
    bwd = [(ring[p], ring[(p - 1) % n]) for p in range(n)]

    def table(shift, sign):
        return jnp.asarray(
            [[ring[(pos[i] + sign * (shift + t)) % n] for i in range(n)] for t in range(n)],
            dtype=jnp.int32,
        )

    fwd_blocks = table(1, -1)
    bwd_blocks = table(1, 1)

    def piece(block, offset, size):
        start = block * rows + offset
        return local(start, size)

    acc_f = piece(fwd_blocks[0, me], 0, half)
    acc_b = piece(bwd_blocks[0, me], half, rows - half)
    for t in range(1, n):
        acc_f = lax.ppermute(acc_f, "sum", fwd) + piece(fwd_blocks[t, me], 0, half)
        acc_b = lax.ppermute(acc_b, "sum", bwd) + piece(bwd_blocks[t, me], half, rows - half)
    return jnp.concatenate([acc_f, acc_b], axis=0)


def ring_gather_carries(own, left_cores, ring):
    n = len(ring)
    rows = own.shape[0]
    half = rows // 2
    pos = [0] * n
    for p, i in enumerate(ring):
        pos[i] = p
    me = lax.axis_index("sum")
    fwd = [(ring[p], ring[(p + 1) % n]) for p in range(n)]
    bwd = [(ring[p], ring[(p - 1) % n]) for p in range(n)]
    fwd_blocks = jnp.asarray(
        [[ring[(pos[i] - t) % n] for i in range(n)] for t in range(n)], dtype=jnp.int32
    )
    bwd_blocks = jnp.asarray(
        [[ring[(pos[i] + t) % n] for i in range(n)] for t in range(n)], dtype=jnp.int32
    )

    def term(piece, block, offset):
        start = block * rows + offset
        lhs = lax.dynamic_slice_in_dim(left_cores, start, piece.shape[0], axis=1)
        return lax.dot_general(
            piece, lhs, (((0, 1), (1, 2)), ((), ())), preferred_element_type=jnp.float32
        )

    hold_f = own[:half]
    hold_b = own[half:]
    total = term(hold_f, fwd_blocks[0, me], 0) + term(hold_b, bwd_blocks[0, me], half)
    for t in range(1, n):
        hold_f = lax.ppermute(hold_f, "sum", fwd)
        hold_b = lax.ppermute(hold_b, "sum", bwd)
        total = total + term(hold_f, fwd_blocks[t, me], 0)
        total = total + term(hold_b, bwd_blocks[t, me], half)
    return jnp.transpose(total, (1, 0, 2))


def per_device(ring, left_cores, right_cores, sketch):
    sum_local, rows_in, mode_local, rank_width = left_cores.shape
    target = sketch.shape[2]
    partial_map = lax.dot_general(
        right_cores, sketch, (((2, 3), (0, 1)), ((), ())), preferred_element_type=jnp.float32
    )
    mapped = lax.psum(partial_map, "mode").astype(jnp.bfloat16)

    def local_rows(start, size):
        part = lax.dynamic_slice_in_dim(left_cores, start, size, axis=1)
        out = lax.dot_general(
            part, mapped, (((0, 3), (0, 1)), ((), ())), preferred_element_type=jnp.float32
        )
        return with_layout_constraint(out, Layout(major_to_minor=(0, 1, 2)))

    factor = math.sqrt(R_IN * MODES)
    share = ring_reduce_scatter(local_rows, rows_in, ring)
    flat_share = share.reshape(-1, target)
    gram_part = jnp.dot(flat_share.T, flat_share, precision=HI)
    gram = symmetric_psum(gram_part)
    basis = orthonormal(flat_share, gram)
    block = basis.reshape(share.shape)
    rounded = block.astype(jnp.bfloat16)
    partial_carry = ring_gather_carries(rounded, left_cores, ring)
    carries = lax.psum(partial_carry, "mode")
    return (block * factor, carries)


def solution(mesh):
    in_specs = (P("sum", None, "mode", None), P("sum", None, "mode", None), P("mode", None, None))
    out_specs = (P("sum", "mode", None), P("sum", None, None))
    ring = ring_order(mesh)
    return jax.shard_map(
        functools.partial(per_device, ring), mesh=mesh, in_specs=in_specs, out_specs=out_specs, check_vma=False
    )
```

```python
import functools
import math

import jax
import jax.numpy as jnp
from jax import lax
from jax.experimental.layout import Layout, with_layout_constraint
from jax.sharding import PartitionSpec as P

R_IN = 512
MODES = 64
BLOCK = 128

HI = lax.Precision.HIGHEST


def mm(a, b):
    return jnp.dot(a, b, precision=HI, preferred_element_type=jnp.float32)


def tri_inverse(lower):
    n = lower.shape[0]
    h = n // 2
    diag = jnp.stack([lower[:h, :h], lower[h:, h:]])
    eye = jnp.broadcast_to(jnp.eye(h, dtype=jnp.float32), diag.shape)
    inv = lax.linalg.triangular_solve(diag, eye, left_side=True, lower=True)
    corner = -mm(inv[1], mm(lower[h:, :h], inv[0]))
    top = jnp.concatenate([inv[0], jnp.zeros((h, n - h), jnp.float32)], axis=1)
    return jnp.concatenate([top, jnp.concatenate([corner, inv[1]], axis=1)], axis=0)


def orthonormal(sketched, gram):
    n = gram.shape[0]
    b = min(BLOCK, n)
    nb = n // b
    eye = jnp.eye(b, dtype=jnp.float32)
    inverses = []
    panels = []
    trailing = gram
    for k in range(nb):
        diag = trailing[:b, :b]
        lkk = jnp.linalg.cholesky(diag)
        ikk = tri_inverse(lkk)
        inverses.append(ikk)
        if k < nb - 1:
            panel = mm(trailing[b:, :b], ikk.T)
            panels.append(panel)
            trailing = trailing[b:, b:] - mm(panel, panel.T)
    blocks = []
    for k in range(nb):
        rhs = sketched[:, k * b:(k + 1) * b]
        if k > 0:
            done = jnp.concatenate(blocks, axis=1)
            lrow = jnp.concatenate(
                [panels[j][(k - j - 1) * b:(k - j) * b] for j in range(k)], axis=1
            )
            rhs = rhs - mm(done, lrow.T)
        blocks.append(mm(rhs, inverses[k].T))
    return jnp.concatenate(blocks, axis=1)


def symmetric_psum(gram_part):
    n = gram_part.shape[0]
    b = min(BLOCK, n)
    nb = n // b
    lower = [(i, j) for i in range(nb) for j in range(i + 1)]
    packed = jnp.stack([gram_part[i * b:(i + 1) * b, j * b:(j + 1) * b] for i, j in lower])
    packed = lax.psum(lax.psum(packed, "mode"), "sum")
    where = {cell: k for k, cell in enumerate(lower)}
    rows = []
    for i in range(nb):
        row = []
        for j in range(nb):
            row.append(packed[where[(i, j)]] if j <= i else packed[where[(j, i)]].T)
        rows.append(jnp.concatenate(row, axis=1))
    return jnp.concatenate(rows, axis=0)


def ring_order(mesh):
    n = mesh.shape["sum"]
    plain = list(range(n))
    try:
        coords = [tuple(int(c) for c in mesh.devices[i, 0].coords) for i in range(n)]
    except (AttributeError, TypeError, IndexError):
        return plain
    axes = [d for d in range(len(coords[0])) if len({c[d] for c in coords}) > 1]
    if len(axes) != 2:
        return plain
    values = [sorted({c[d] for c in coords}) for d in axes]
    if len(values[0]) % 2:
        axes, values = axes[::-1], values[::-1]
    if len(values[0]) % 2 or len(values[0]) * len(values[1]) != n:
        return plain
    where = {(c[axes[0]], c[axes[1]]): i for i, c in enumerate(coords)}
    first, second = values
    cells = [(a, second[0]) for a in first]
    for row, a in enumerate(reversed(first)):
        cols = second[1:] if row % 2 == 0 else second[1:][::-1]
        cells.extend((a, b) for b in cols)
    if len(set(cells)) != n or any(cell not in where for cell in cells):
        return plain
    return [where[cell] for cell in cells]


def ring_reduce_scatter(local, total_rows, ring):
    n = len(ring)
    rows = total_rows // n
    half = rows // 2
    pos = [0] * n
    for p, i in enumerate(ring):
        pos[i] = p
    me = lax.axis_index("sum")
    fwd = [(ring[p], ring[(p + 1) % n]) for p in range(n)]
    bwd = [(ring[p], ring[(p - 1) % n]) for p in range(n)]

    def table(shift, sign):
        return jnp.asarray(
            [[ring[(pos[i] + sign * (shift + t)) % n] for i in range(n)] for t in range(n)],
            dtype=jnp.int32,
        )

    fwd_blocks = table(1, -1)
    bwd_blocks = table(1, 1)

    def piece(block, offset, size):
        start = block * rows + offset
        return local(start, size)

    acc_f = piece(fwd_blocks[0, me], 0, half)
    acc_b = piece(bwd_blocks[0, me], half, rows - half)
    for t in range(1, n):
        acc_f = lax.ppermute(acc_f, "sum", fwd) + piece(fwd_blocks[t, me], 0, half)
        acc_b = lax.ppermute(acc_b, "sum", bwd) + piece(bwd_blocks[t, me], half, rows - half)
    return jnp.concatenate([acc_f, acc_b], axis=0)


def ring_gather_carries(own, left_cores, ring):
    n = len(ring)
    rows = own.shape[0]
    half = rows // 2
    pos = [0] * n
    for p, i in enumerate(ring):
        pos[i] = p
    me = lax.axis_index("sum")
    fwd = [(ring[p], ring[(p + 1) % n]) for p in range(n)]
    bwd = [(ring[p], ring[(p - 1) % n]) for p in range(n)]
    fwd_blocks = jnp.asarray(
        [[ring[(pos[i] - t) % n] for i in range(n)] for t in range(n)], dtype=jnp.int32
    )
    bwd_blocks = jnp.asarray(
        [[ring[(pos[i] + t) % n] for i in range(n)] for t in range(n)], dtype=jnp.int32
    )

    def term(piece, block, offset):
        start = block * rows + offset
        lhs = lax.dynamic_slice_in_dim(left_cores, start, piece.shape[0], axis=1)
        return lax.dot_general(
            piece, lhs, (((0, 1), (1, 2)), ((), ())), preferred_element_type=jnp.float32
        )

    hold_f = own[:half]
    hold_b = own[half:]
    total = term(hold_f, fwd_blocks[0, me], 0) + term(hold_b, bwd_blocks[0, me], half)
    for t in range(1, n):
        hold_f = lax.ppermute(hold_f, "sum", fwd)
        hold_b = lax.ppermute(hold_b, "sum", bwd)
        total = total + term(hold_f, fwd_blocks[t, me], 0)
        total = total + term(hold_b, bwd_blocks[t, me], half)
    return jnp.transpose(total, (1, 0, 2))


def per_device(ring, left_cores, right_cores, sketch):
    sum_local, rows_in, mode_local, rank_width = left_cores.shape
    target = sketch.shape[2]
    partial_map = lax.dot_general(
        right_cores, sketch, (((2, 3), (0, 1)), ((), ())), preferred_element_type=jnp.float32
    )
    mapped = lax.psum(partial_map, "mode").astype(jnp.bfloat16)

    def local_rows(start, size):
        part = lax.dynamic_slice_in_dim(left_cores, start, size, axis=1)
        out = lax.dot_general(
            part, mapped, (((0, 3), (0, 1)), ((), ())), preferred_element_type=jnp.float32
        )
        return with_layout_constraint(out, Layout(major_to_minor=(0, 1, 2)))

    factor = math.sqrt(R_IN * MODES)
    share = ring_reduce_scatter(local_rows, rows_in, ring)
    flat_share = share.reshape(-1, target)
    gram_part = jnp.dot(flat_share.T, flat_share, precision=HI)
    gram = symmetric_psum(gram_part)
    basis = orthonormal(flat_share, gram)
    block = basis.reshape(share.shape)
    rounded = block.astype(jnp.bfloat16)
    partial_carry = ring_gather_carries(rounded, left_cores, ring)
    carries = lax.psum(partial_carry, "mode")
    return (block * factor, carries)


def solution(mesh):
    in_specs = (P("sum", None, "mode", None), P("sum", None, "mode", None), P("mode", None, None))
    out_specs = (P("sum", "mode", None), P("sum", None, None))
    ring = ring_order(mesh)
    return jax.shard_map(
        functools.partial(per_device, ring), mesh=mesh, in_specs=in_specs, out_specs=out_specs, check_vma=False
    )
```

```python
import functools
import math

import jax
import jax.numpy as jnp
from jax import lax
from jax.experimental.layout import Layout, with_layout_constraint
from jax.sharding import PartitionSpec as P

R_IN = 512
MODES = 64
BLOCK = 128

HI = lax.Precision.HIGHEST


def mm(a, b):
    return jnp.dot(a, b, precision=HI, preferred_element_type=jnp.float32)


def tri_inverse(lower):
    n = lower.shape[0]
    h = n // 2
    diag = jnp.stack([lower[:h, :h], lower[h:, h:]])
    eye = jnp.broadcast_to(jnp.eye(h, dtype=jnp.float32), diag.shape)
    inv = lax.linalg.triangular_solve(diag, eye, left_side=True, lower=True)
    corner = -mm(inv[1], mm(lower[h:, :h], inv[0]))
    top = jnp.concatenate([inv[0], jnp.zeros((h, n - h), jnp.float32)], axis=1)
    return jnp.concatenate([top, jnp.concatenate([corner, inv[1]], axis=1)], axis=0)


def orthonormal(sketched, gram):
    n = gram.shape[0]
    b = min(BLOCK, n)
    nb = n // b
    eye = jnp.eye(b, dtype=jnp.float32)
    inverses = []
    panels = []
    trailing = gram
    for k in range(nb):
        diag = trailing[:b, :b]
        lkk = jnp.linalg.cholesky(diag)
        ikk = tri_inverse(lkk)
        inverses.append(ikk)
        if k < nb - 1:
            panel = mm(trailing[b:, :b], ikk.T)
            panels.append(panel)
            trailing = trailing[b:, b:] - mm(panel, panel.T)
    blocks = []
    for k in range(nb):
        rhs = sketched[:, k * b:(k + 1) * b]
        if k > 0:
            done = jnp.concatenate(blocks, axis=1)
            lrow = jnp.concatenate(
                [panels[j][(k - j - 1) * b:(k - j) * b] for j in range(k)], axis=1
            )
            rhs = rhs - mm(done, lrow.T)
        blocks.append(mm(rhs, inverses[k].T))
    return jnp.concatenate(blocks, axis=1)


def butterfly_sum(x, n):
    if n & (n - 1):
        return lax.psum(x, "sum")
    d = 1
    while d < n:
        x = x + lax.ppermute(x, "sum", [(i, i ^ d) for i in range(n)])
        d *= 2
    return x


def symmetric_psum(gram_part, n_sum):
    n = gram_part.shape[0]
    b = min(BLOCK, n)
    nb = n // b
    lower = [(i, j) for i in range(nb) for j in range(i + 1)]
    packed = jnp.stack([gram_part[i * b:(i + 1) * b, j * b:(j + 1) * b] for i, j in lower])
    packed = butterfly_sum(lax.psum(packed, "mode"), n_sum)
    where = {cell: k for k, cell in enumerate(lower)}
    rows = []
    for i in range(nb):
        row = []
        for j in range(nb):
            row.append(packed[where[(i, j)]] if j <= i else packed[where[(j, i)]].T)
        rows.append(jnp.concatenate(row, axis=1))
    return jnp.concatenate(rows, axis=0)


def ring_order(mesh):
    n = mesh.shape["sum"]
    plain = list(range(n))
    try:
        coords = [tuple(int(c) for c in mesh.devices[i, 0].coords) for i in range(n)]
    except (AttributeError, TypeError, IndexError):
        return plain
    axes = [d for d in range(len(coords[0])) if len({c[d] for c in coords}) > 1]
    if len(axes) != 2:
        return plain
    values = [sorted({c[d] for c in coords}) for d in axes]
    if len(values[0]) % 2:
        axes, values = axes[::-1], values[::-1]
    if len(values[0]) % 2 or len(values[0]) * len(values[1]) != n:
        return plain
    where = {(c[axes[0]], c[axes[1]]): i for i, c in enumerate(coords)}
    first, second = values
    cells = [(a, second[0]) for a in first]
    for row, a in enumerate(reversed(first)):
        cols = second[1:] if row % 2 == 0 else second[1:][::-1]
        cells.extend((a, b) for b in cols)
    if len(set(cells)) != n or any(cell not in where for cell in cells):
        return plain
    return [where[cell] for cell in cells]


def ring_reduce_scatter(local, total_rows, ring):
    n = len(ring)
    rows = total_rows // n
    half = rows // 2
    pos = [0] * n
    for p, i in enumerate(ring):
        pos[i] = p
    me = lax.axis_index("sum")
    fwd = [(ring[p], ring[(p + 1) % n]) for p in range(n)]
    bwd = [(ring[p], ring[(p - 1) % n]) for p in range(n)]

    def table(shift, sign):
        return jnp.asarray(
            [[ring[(pos[i] + sign * (shift + t)) % n] for i in range(n)] for t in range(n)],
            dtype=jnp.int32,
        )

    fwd_blocks = table(1, -1)
    bwd_blocks = table(1, 1)

    def piece(block, offset, size):
        start = block * rows + offset
        return local(start, size)

    acc_f = piece(fwd_blocks[0, me], 0, half)
    acc_b = piece(bwd_blocks[0, me], half, rows - half)
    for t in range(1, n):
        acc_f = lax.ppermute(acc_f, "sum", fwd) + piece(fwd_blocks[t, me], 0, half)
        acc_b = lax.ppermute(acc_b, "sum", bwd) + piece(bwd_blocks[t, me], half, rows - half)
    return jnp.concatenate([acc_f, acc_b], axis=0)


def ring_gather_carries(own, left_cores, ring):
    n = len(ring)
    rows = own.shape[0]
    half = rows // 2
    pos = [0] * n
    for p, i in enumerate(ring):
        pos[i] = p
    me = lax.axis_index("sum")
    fwd = [(ring[p], ring[(p + 1) % n]) for p in range(n)]
    bwd = [(ring[p], ring[(p - 1) % n]) for p in range(n)]
    fwd_blocks = jnp.asarray(
        [[ring[(pos[i] - t) % n] for i in range(n)] for t in range(n)], dtype=jnp.int32
    )
    bwd_blocks = jnp.asarray(
        [[ring[(pos[i] + t) % n] for i in range(n)] for t in range(n)], dtype=jnp.int32
    )

    def term(piece, block, offset):
        start = block * rows + offset
        lhs = lax.dynamic_slice_in_dim(left_cores, start, piece.shape[0], axis=1)
        return lax.dot_general(
            piece, lhs, (((0, 1), (1, 2)), ((), ())), preferred_element_type=jnp.float32
        )

    hold_f = own[:half]
    hold_b = own[half:]
    total = term(hold_f, fwd_blocks[0, me], 0) + term(hold_b, bwd_blocks[0, me], half)
    for t in range(1, n):
        hold_f = lax.ppermute(hold_f, "sum", fwd)
        hold_b = lax.ppermute(hold_b, "sum", bwd)
        total = total + term(hold_f, fwd_blocks[t, me], 0)
        total = total + term(hold_b, bwd_blocks[t, me], half)
    return jnp.transpose(total, (1, 0, 2))


def per_device(ring, left_cores, right_cores, sketch):
    sum_local, rows_in, mode_local, rank_width = left_cores.shape
    target = sketch.shape[2]
    partial_map = lax.dot_general(
        right_cores, sketch, (((2, 3), (0, 1)), ((), ())), preferred_element_type=jnp.float32
    )
    mapped = lax.psum(partial_map, "mode").astype(jnp.bfloat16)

    def local_rows(start, size):
        part = lax.dynamic_slice_in_dim(left_cores, start, size, axis=1)
        out = lax.dot_general(
            part, mapped, (((0, 3), (0, 1)), ((), ())), preferred_element_type=jnp.float32
        )
        return with_layout_constraint(out, Layout(major_to_minor=(0, 1, 2)))

    factor = math.sqrt(R_IN * MODES)
    share = ring_reduce_scatter(local_rows, rows_in, ring)
    flat_share = share.reshape(-1, target)
    gram_part = jnp.dot(flat_share.T, flat_share, precision=HI)
    gram = symmetric_psum(gram_part, len(ring))
    basis = orthonormal(flat_share, gram)
    block = basis.reshape(share.shape)
    rounded = block.astype(jnp.bfloat16)
    partial_carry = ring_gather_carries(rounded, left_cores, ring)
    carries = lax.psum(partial_carry, "mode")
    return (block * factor, carries)


def solution(mesh):
    in_specs = (P("sum", None, "mode", None), P("sum", None, "mode", None), P("mode", None, None))
    out_specs = (P("sum", "mode", None), P("sum", None, None))
    ring = ring_order(mesh)
    return jax.shard_map(
        functools.partial(per_device, ring), mesh=mesh, in_specs=in_specs, out_specs=out_specs, check_vma=False
    )
```

```python
import functools
import math

import jax
import jax.numpy as jnp
from jax import lax
from jax.experimental.layout import Layout, with_layout_constraint
from jax.sharding import PartitionSpec as P

R_IN = 512
MODES = 64
BLOCK = 128

HI = lax.Precision.HIGHEST


def mm(a, b):
    return jnp.dot(a, b, precision=HI, preferred_element_type=jnp.float32)


def tri_inverse(lower):
    n = lower.shape[0]
    h = n // 2
    diag = jnp.stack([lower[:h, :h], lower[h:, h:]])
    eye = jnp.broadcast_to(jnp.eye(h, dtype=jnp.float32), diag.shape)
    inv = lax.linalg.triangular_solve(diag, eye, left_side=True, lower=True)
    corner = -mm(inv[1], mm(lower[h:, :h], inv[0]))
    top = jnp.concatenate([inv[0], jnp.zeros((h, n - h), jnp.float32)], axis=1)
    return jnp.concatenate([top, jnp.concatenate([corner, inv[1]], axis=1)], axis=0)


def orthonormal(sketched, gram):
    n = gram.shape[0]
    b = min(BLOCK, n)
    nb = n // b
    eye = jnp.eye(b, dtype=jnp.float32)
    inverses = []
    panels = []
    trailing = gram
    for k in range(nb):
        diag = trailing[:b, :b]
        lkk = jnp.linalg.cholesky(diag)
        ikk = tri_inverse(lkk)
        inverses.append(ikk)
        if k < nb - 1:
            panel = mm(trailing[b:, :b], ikk.T)
            panels.append(panel)
            trailing = trailing[b:, b:] - mm(panel, panel.T)
    blocks = []
    for k in range(nb):
        rhs = sketched[:, k * b:(k + 1) * b]
        if k > 0:
            done = jnp.concatenate(blocks, axis=1)
            lrow = jnp.concatenate(
                [panels[j][(k - j - 1) * b:(k - j) * b] for j in range(k)], axis=1
            )
            rhs = rhs - mm(done, lrow.T)
        blocks.append(mm(rhs, inverses[k].T))
    return jnp.concatenate(blocks, axis=1)


def butterfly_sum(x, n, axis="sum"):
    if n & (n - 1):
        return lax.psum(x, axis)
    d = 1
    while d < n:
        x = x + lax.ppermute(x, axis, [(i, i ^ d) for i in range(n)])
        d *= 2
    return x


def symmetric_psum(gram_part, n_sum, n_mode):
    n = gram_part.shape[0]
    b = min(BLOCK, n)
    nb = n // b
    lower = [(i, j) for i in range(nb) for j in range(i + 1)]
    packed = jnp.stack([gram_part[i * b:(i + 1) * b, j * b:(j + 1) * b] for i, j in lower])
    packed = butterfly_sum(butterfly_sum(packed, n_mode, "mode"), n_sum)
    where = {cell: k for k, cell in enumerate(lower)}
    rows = []
    for i in range(nb):
        row = []
        for j in range(nb):
            row.append(packed[where[(i, j)]] if j <= i else packed[where[(j, i)]].T)
        rows.append(jnp.concatenate(row, axis=1))
    return jnp.concatenate(rows, axis=0)


def ring_order(mesh):
    n = mesh.shape["sum"]
    plain = list(range(n))
    try:
        coords = [tuple(int(c) for c in mesh.devices[i, 0].coords) for i in range(n)]
    except (AttributeError, TypeError, IndexError):
        return plain
    axes = [d for d in range(len(coords[0])) if len({c[d] for c in coords}) > 1]
    if len(axes) != 2:
        return plain
    values = [sorted({c[d] for c in coords}) for d in axes]
    if len(values[0]) % 2:
        axes, values = axes[::-1], values[::-1]
    if len(values[0]) % 2 or len(values[0]) * len(values[1]) != n:
        return plain
    where = {(c[axes[0]], c[axes[1]]): i for i, c in enumerate(coords)}
    first, second = values
    cells = [(a, second[0]) for a in first]
    for row, a in enumerate(reversed(first)):
        cols = second[1:] if row % 2 == 0 else second[1:][::-1]
        cells.extend((a, b) for b in cols)
    if len(set(cells)) != n or any(cell not in where for cell in cells):
        return plain
    return [where[cell] for cell in cells]


def ring_reduce_scatter(local, total_rows, ring):
    n = len(ring)
    rows = total_rows // n
    half = rows // 2
    pos = [0] * n
    for p, i in enumerate(ring):
        pos[i] = p
    me = lax.axis_index("sum")
    fwd = [(ring[p], ring[(p + 1) % n]) for p in range(n)]
    bwd = [(ring[p], ring[(p - 1) % n]) for p in range(n)]

    def table(shift, sign):
        return jnp.asarray(
            [[ring[(pos[i] + sign * (shift + t)) % n] for i in range(n)] for t in range(n)],
            dtype=jnp.int32,
        )

    fwd_blocks = table(1, -1)
    bwd_blocks = table(1, 1)

    def piece(block, offset, size):
        start = block * rows + offset
        return local(start, size)

    acc_f = piece(fwd_blocks[0, me], 0, half)
    acc_b = piece(bwd_blocks[0, me], half, rows - half)
    for t in range(1, n):
        acc_f = lax.ppermute(acc_f, "sum", fwd) + piece(fwd_blocks[t, me], 0, half)
        acc_b = lax.ppermute(acc_b, "sum", bwd) + piece(bwd_blocks[t, me], half, rows - half)
    return jnp.concatenate([acc_f, acc_b], axis=0)


def ring_gather_carries(own, left_cores, ring):
    n = len(ring)
    rows = own.shape[0]
    half = rows // 2
    pos = [0] * n
    for p, i in enumerate(ring):
        pos[i] = p
    me = lax.axis_index("sum")
    fwd = [(ring[p], ring[(p + 1) % n]) for p in range(n)]
    bwd = [(ring[p], ring[(p - 1) % n]) for p in range(n)]
    fwd_blocks = jnp.asarray(
        [[ring[(pos[i] - t) % n] for i in range(n)] for t in range(n)], dtype=jnp.int32
    )
    bwd_blocks = jnp.asarray(
        [[ring[(pos[i] + t) % n] for i in range(n)] for t in range(n)], dtype=jnp.int32
    )

    def term(piece, block, offset):
        start = block * rows + offset
        lhs = lax.dynamic_slice_in_dim(left_cores, start, piece.shape[0], axis=1)
        return lax.dot_general(
            piece, lhs, (((0, 1), (1, 2)), ((), ())), preferred_element_type=jnp.float32
        )

    hold_f = own[:half]
    hold_b = own[half:]
    total = term(hold_f, fwd_blocks[0, me], 0) + term(hold_b, bwd_blocks[0, me], half)
    for t in range(1, n):
        hold_f = lax.ppermute(hold_f, "sum", fwd)
        hold_b = lax.ppermute(hold_b, "sum", bwd)
        total = total + term(hold_f, fwd_blocks[t, me], 0)
        total = total + term(hold_b, bwd_blocks[t, me], half)
    return jnp.transpose(total, (1, 0, 2))


def per_device(ring, n_mode, left_cores, right_cores, sketch):
    sum_local, rows_in, mode_local, rank_width = left_cores.shape
    target = sketch.shape[2]
    partial_map = lax.dot_general(
        right_cores, sketch, (((2, 3), (0, 1)), ((), ())), preferred_element_type=jnp.float32
    )
    mapped = lax.psum(partial_map, "mode").astype(jnp.bfloat16)

    def local_rows(start, size):
        part = lax.dynamic_slice_in_dim(left_cores, start, size, axis=1)
        out = lax.dot_general(
            part, mapped, (((0, 3), (0, 1)), ((), ())), preferred_element_type=jnp.float32
        )
        return with_layout_constraint(out, Layout(major_to_minor=(0, 1, 2)))

    factor = math.sqrt(R_IN * MODES)
    share = ring_reduce_scatter(local_rows, rows_in, ring)
    flat_share = share.reshape(-1, target)
    gram_part = jnp.dot(flat_share.T, flat_share, precision=HI)
    gram = symmetric_psum(gram_part, len(ring), n_mode)
    basis = orthonormal(flat_share, gram)
    block = basis.reshape(share.shape)
    rounded = block.astype(jnp.bfloat16)
    partial_carry = ring_gather_carries(rounded, left_cores, ring)
    carries = butterfly_sum(partial_carry, n_mode, "mode")
    return (block * factor, carries)


def solution(mesh):
    in_specs = (P("sum", None, "mode", None), P("sum", None, "mode", None), P("mode", None, None))
    out_specs = (P("sum", "mode", None), P("sum", None, None))
    ring = ring_order(mesh)
    return jax.shard_map(
        functools.partial(per_device, ring, mesh.shape["mode"]), mesh=mesh, in_specs=in_specs, out_specs=out_specs, check_vma=False
    )
```

```python
import functools
import math

import jax
import jax.numpy as jnp
from jax import lax
from jax.experimental.layout import Layout, with_layout_constraint
from jax.sharding import PartitionSpec as P

R_IN = 512
MODES = 64
BLOCK = 128

HI = lax.Precision.HIGHEST


def mm(a, b):
    return jnp.dot(a, b, precision=HI, preferred_element_type=jnp.float32)


def tri_inverse(lower):
    n = lower.shape[0]
    h = n // 2
    diag = jnp.stack([lower[:h, :h], lower[h:, h:]])
    eye = jnp.broadcast_to(jnp.eye(h, dtype=jnp.float32), diag.shape)
    inv = lax.linalg.triangular_solve(diag, eye, left_side=True, lower=True)
    corner = -mm(inv[1], mm(lower[h:, :h], inv[0]))
    top = jnp.concatenate([inv[0], jnp.zeros((h, n - h), jnp.float32)], axis=1)
    return jnp.concatenate([top, jnp.concatenate([corner, inv[1]], axis=1)], axis=0)


def orthonormal(sketched, gram):
    n = gram.shape[0]
    b = min(BLOCK, n)
    nb = n // b
    eye = jnp.eye(b, dtype=jnp.float32)
    inverses = []
    panels = []
    trailing = gram
    for k in range(nb):
        diag = trailing[:b, :b]
        lkk = jnp.linalg.cholesky(diag)
        ikk = tri_inverse(lkk)
        inverses.append(ikk)
        if k < nb - 1:
            panel = mm(trailing[b:, :b], ikk.T)
            panels.append(panel)
            trailing = trailing[b:, b:] - mm(panel, panel.T)
    blocks = []
    for k in range(nb):
        rhs = sketched[:, k * b:(k + 1) * b]
        if k > 0:
            done = jnp.concatenate(blocks, axis=1)
            lrow = jnp.concatenate(
                [panels[j][(k - j - 1) * b:(k - j) * b] for j in range(k)], axis=1
            )
            rhs = rhs - mm(done, lrow.T)
        blocks.append(mm(rhs, inverses[k].T))
    return jnp.concatenate(blocks, axis=1)


def butterfly_sum(x, n, axis="sum"):
    if n & (n - 1):
        return lax.psum(x, axis)
    d = 1
    while d < n:
        x = x + lax.ppermute(x, axis, [(i, i ^ d) for i in range(n)])
        d *= 2
    return x


def symmetric_psum(gram_part, n_sum, n_mode):
    n = gram_part.shape[0]
    b = min(BLOCK, n)
    nb = n // b
    lower = [(i, j) for i in range(nb) for j in range(i + 1)]
    packed = jnp.stack([gram_part[i * b:(i + 1) * b, j * b:(j + 1) * b] for i, j in lower])
    packed = butterfly_sum(butterfly_sum(packed, n_mode, "mode"), n_sum)
    where = {cell: k for k, cell in enumerate(lower)}
    rows = []
    for i in range(nb):
        row = []
        for j in range(nb):
            row.append(packed[where[(i, j)]] if j <= i else packed[where[(j, i)]].T)
        rows.append(jnp.concatenate(row, axis=1))
    return jnp.concatenate(rows, axis=0)


def ring_order(mesh):
    n = mesh.shape["sum"]
    plain = list(range(n))
    try:
        coords = [tuple(int(c) for c in mesh.devices[i, 0].coords) for i in range(n)]
    except (AttributeError, TypeError, IndexError):
        return plain
    axes = [d for d in range(len(coords[0])) if len({c[d] for c in coords}) > 1]
    if len(axes) != 2:
        return plain
    values = [sorted({c[d] for c in coords}) for d in axes]
    if len(values[0]) % 2:
        axes, values = axes[::-1], values[::-1]
    if len(values[0]) % 2 or len(values[0]) * len(values[1]) != n:
        return plain
    where = {(c[axes[0]], c[axes[1]]): i for i, c in enumerate(coords)}
    first, second = values
    cells = [(a, second[0]) for a in first]
    for row, a in enumerate(reversed(first)):
        cols = second[1:] if row % 2 == 0 else second[1:][::-1]
        cells.extend((a, b) for b in cols)
    if len(set(cells)) != n or any(cell not in where for cell in cells):
        return plain
    return [where[cell] for cell in cells]


def ring_reduce_scatter(local, total_rows, ring):
    n = len(ring)
    rows = total_rows // n
    half = rows // 2
    pos = [0] * n
    for p, i in enumerate(ring):
        pos[i] = p
    me = lax.axis_index("sum")
    fwd = [(ring[p], ring[(p + 1) % n]) for p in range(n)]
    bwd = [(ring[p], ring[(p - 1) % n]) for p in range(n)]

    def table(shift, sign):
        return jnp.asarray(
            [[ring[(pos[i] + sign * (shift + t)) % n] for i in range(n)] for t in range(n)],
            dtype=jnp.int32,
        )

    fwd_blocks = table(1, -1)
    bwd_blocks = table(1, 1)

    def piece(block, offset, size):
        start = block * rows + offset
        return local(start, size)

    acc_f = piece(fwd_blocks[0, me], 0, half)
    acc_b = piece(bwd_blocks[0, me], half, rows - half)
    for t in range(1, n):
        acc_f = lax.ppermute(acc_f, "sum", fwd) + piece(fwd_blocks[t, me], 0, half)
        acc_b = lax.ppermute(acc_b, "sum", bwd) + piece(bwd_blocks[t, me], half, rows - half)
    return jnp.concatenate([acc_f, acc_b], axis=0)


def ring_gather_carries(own, left_cores, ring):
    n = len(ring)
    rows = own.shape[0]
    half = rows // 2
    pos = [0] * n
    for p, i in enumerate(ring):
        pos[i] = p
    me = lax.axis_index("sum")
    fwd = [(ring[p], ring[(p + 1) % n]) for p in range(n)]
    bwd = [(ring[p], ring[(p - 1) % n]) for p in range(n)]
    fwd_blocks = jnp.asarray(
        [[ring[(pos[i] - t) % n] for i in range(n)] for t in range(n)], dtype=jnp.int32
    )
    bwd_blocks = jnp.asarray(
        [[ring[(pos[i] + t) % n] for i in range(n)] for t in range(n)], dtype=jnp.int32
    )

    def term(piece, block, offset):
        start = block * rows + offset
        lhs = lax.dynamic_slice_in_dim(left_cores, start, piece.shape[0], axis=1)
        return lax.dot_general(
            piece, lhs, (((0, 1), (1, 2)), ((), ())), preferred_element_type=jnp.float32
        )

    hold_f = own[:half]
    hold_b = own[half:]
    total = term(hold_f, fwd_blocks[0, me], 0) + term(hold_b, bwd_blocks[0, me], half)
    for t in range(1, n):
        hold_f = lax.ppermute(hold_f, "sum", fwd)
        hold_b = lax.ppermute(hold_b, "sum", bwd)
        total = total + term(hold_f, fwd_blocks[t, me], 0)
        total = total + term(hold_b, bwd_blocks[t, me], half)
    return jnp.transpose(total, (1, 0, 2))


def per_device(ring, n_mode, left_cores, right_cores, sketch):
    sum_local, rows_in, mode_local, rank_width = left_cores.shape
    target = sketch.shape[2]
    partial_map = lax.dot_general(
        right_cores, sketch, (((2, 3), (0, 1)), ((), ())), preferred_element_type=jnp.float32
    )
    mapped = butterfly_sum(partial_map, n_mode, "mode").astype(jnp.bfloat16)

    def local_rows(start, size):
        part = lax.dynamic_slice_in_dim(left_cores, start, size, axis=1)
        out = lax.dot_general(
            part, mapped, (((0, 3), (0, 1)), ((), ())), preferred_element_type=jnp.float32
        )
        return with_layout_constraint(out, Layout(major_to_minor=(0, 1, 2)))

    factor = math.sqrt(R_IN * MODES)
    share = ring_reduce_scatter(local_rows, rows_in, ring)
    flat_share = share.reshape(-1, target)
    gram_part = jnp.dot(flat_share.T, flat_share, precision=HI)
    gram = symmetric_psum(gram_part, len(ring), n_mode)
    basis = orthonormal(flat_share, gram)
    block = basis.reshape(share.shape)
    rounded = block.astype(jnp.bfloat16)
    partial_carry = ring_gather_carries(rounded, left_cores, ring)
    carries = butterfly_sum(partial_carry, n_mode, "mode")
    return (block * factor, carries)


def solution(mesh):
    in_specs = (P("sum", None, "mode", None), P("sum", None, "mode", None), P("mode", None, None))
    out_specs = (P("sum", "mode", None), P("sum", None, None))
    ring = ring_order(mesh)
    return jax.shard_map(
        functools.partial(per_device, ring, mesh.shape["mode"]), mesh=mesh, in_specs=in_specs, out_specs=out_specs, check_vma=False
    )
```

```python
import functools
import math

import jax
import jax.numpy as jnp
from jax import lax
from jax.experimental.layout import Layout, with_layout_constraint
from jax.sharding import PartitionSpec as P

R_IN = 512
MODES = 64
BLOCK = 128

HI = lax.Precision.HIGHEST


def mm(a, b):
    return jnp.dot(a, b, precision=HI, preferred_element_type=jnp.float32)


def tri_inverse(lower):
    n = lower.shape[0]
    h = n // 2
    diag = jnp.stack([lower[:h, :h], lower[h:, h:]])
    eye = jnp.broadcast_to(jnp.eye(h, dtype=jnp.float32), diag.shape)
    inv = lax.linalg.triangular_solve(diag, eye, left_side=True, lower=True)
    corner = -mm(inv[1], mm(lower[h:, :h], inv[0]))
    top = jnp.concatenate([inv[0], jnp.zeros((h, n - h), jnp.float32)], axis=1)
    return jnp.concatenate([top, jnp.concatenate([corner, inv[1]], axis=1)], axis=0)


def orthonormal(sketched, gram):
    n = gram.shape[0]
    b = min(BLOCK, n)
    nb = n // b
    eye = jnp.eye(b, dtype=jnp.float32)
    inverses = []
    panels = []
    trailing = gram
    for k in range(nb):
        diag = trailing[:b, :b]
        lkk = jnp.linalg.cholesky(diag)
        ikk = tri_inverse(lkk)
        inverses.append(ikk)
        if k < nb - 1:
            panel = mm(trailing[b:, :b], ikk.T)
            panels.append(panel)
            trailing = trailing[b:, b:] - mm(panel, panel.T)
    blocks = []
    for k in range(nb):
        rhs = sketched[:, k * b:(k + 1) * b]
        if k > 0:
            done = jnp.concatenate(blocks, axis=1)
            lrow = jnp.concatenate(
                [panels[j][(k - j - 1) * b:(k - j) * b] for j in range(k)], axis=1
            )
            rhs = rhs - mm(done, lrow.T)
        blocks.append(mm(rhs, inverses[k].T))
    return jnp.concatenate(blocks, axis=1)


def butterfly_sum(x, n, axis="sum"):
    if n & (n - 1):
        return lax.psum(x, axis)
    d = 1
    while d < n:
        x = x + lax.ppermute(x, axis, [(i, i ^ d) for i in range(n)])
        d *= 2
    return x


def symmetric_psum(gram_part, n_sum, n_mode):
    n = gram_part.shape[0]
    b = min(BLOCK, n)
    nb = n // b
    lower = [(i, j) for i in range(nb) for j in range(i + 1)]
    packed = jnp.stack([gram_part[i * b:(i + 1) * b, j * b:(j + 1) * b] for i, j in lower])
    packed = butterfly_sum(butterfly_sum(packed, n_mode, "mode"), n_sum)
    where = {cell: k for k, cell in enumerate(lower)}
    rows = []
    for i in range(nb):
        row = []
        for j in range(nb):
            row.append(packed[where[(i, j)]] if j <= i else packed[where[(j, i)]].T)
        rows.append(jnp.concatenate(row, axis=1))
    return jnp.concatenate(rows, axis=0)


def ring_order(mesh):
    n = mesh.shape["sum"]
    plain = list(range(n))
    try:
        coords = [tuple(int(c) for c in mesh.devices[i, 0].coords) for i in range(n)]
    except (AttributeError, TypeError, IndexError):
        return plain
    axes = [d for d in range(len(coords[0])) if len({c[d] for c in coords}) > 1]
    if len(axes) != 2:
        return plain
    values = [sorted({c[d] for c in coords}) for d in axes]
    if len(values[0]) % 2:
        axes, values = axes[::-1], values[::-1]
    if len(values[0]) % 2 or len(values[0]) * len(values[1]) != n:
        return plain
    where = {(c[axes[0]], c[axes[1]]): i for i, c in enumerate(coords)}
    first, second = values
    cells = [(a, second[0]) for a in first]
    for row, a in enumerate(reversed(first)):
        cols = second[1:] if row % 2 == 0 else second[1:][::-1]
        cells.extend((a, b) for b in cols)
    if len(set(cells)) != n or any(cell not in where for cell in cells):
        return plain
    return [where[cell] for cell in cells]


def ring_reduce_scatter(local, total_rows, ring):
    n = len(ring)
    rows = total_rows // n
    half = rows // 2
    pos = [0] * n
    for p, i in enumerate(ring):
        pos[i] = p
    me = lax.axis_index("sum")
    fwd = [(ring[p], ring[(p + 1) % n]) for p in range(n)]
    bwd = [(ring[p], ring[(p - 1) % n]) for p in range(n)]

    def table(shift, sign):
        return jnp.asarray(
            [[ring[(pos[i] + sign * (shift + t)) % n] for i in range(n)] for t in range(n)],
            dtype=jnp.int32,
        )

    fwd_blocks = table(1, -1)
    bwd_blocks = table(1, 1)

    def piece(block, offset, size):
        start = block * rows + offset
        return local(start, size)

    acc_f = piece(fwd_blocks[0, me], 0, half)
    acc_b = piece(bwd_blocks[0, me], half, rows - half)
    for t in range(1, n):
        acc_f = lax.ppermute(acc_f, "sum", fwd) + piece(fwd_blocks[t, me], 0, half)
        acc_b = lax.ppermute(acc_b, "sum", bwd) + piece(bwd_blocks[t, me], half, rows - half)
    return jnp.concatenate([acc_f, acc_b], axis=0)


def ring_gather_carries(own, left_cores, ring):
    n = len(ring)
    rows = own.shape[0]
    half = rows // 2
    pos = [0] * n
    for p, i in enumerate(ring):
        pos[i] = p
    me = lax.axis_index("sum")
    fwd = [(ring[p], ring[(p + 1) % n]) for p in range(n)]
    bwd = [(ring[p], ring[(p - 1) % n]) for p in range(n)]
    fwd_blocks = jnp.asarray(
        [[ring[(pos[i] - t) % n] for i in range(n)] for t in range(n)], dtype=jnp.int32
    )
    bwd_blocks = jnp.asarray(
        [[ring[(pos[i] + t) % n] for i in range(n)] for t in range(n)], dtype=jnp.int32
    )

    def term(piece, block, offset):
        start = block * rows + offset
        lhs = lax.dynamic_slice_in_dim(left_cores, start, piece.shape[0], axis=1)
        return lax.dot_general(
            piece, lhs, (((0, 1), (1, 2)), ((), ())), preferred_element_type=jnp.float32
        )

    hold_f = own[:half]
    hold_b = own[half:]
    total = term(hold_f, fwd_blocks[0, me], 0) + term(hold_b, bwd_blocks[0, me], half)
    for t in range(1, n):
        hold_f = lax.ppermute(hold_f, "sum", fwd)
        hold_b = lax.ppermute(hold_b, "sum", bwd)
        total = total + term(hold_f, fwd_blocks[t, me], 0)
        total = total + term(hold_b, bwd_blocks[t, me], half)
    return jnp.transpose(total, (1, 0, 2))


def per_device(ring, n_mode, left_cores, right_cores, sketch):
    sum_local, rows_in, mode_local, rank_width = left_cores.shape
    target = sketch.shape[2]
    cut = rank_width // 2
    halves = []
    for lo, hi in ((0, cut), (cut, rank_width)):
        part = lax.dot_general(
            right_cores[:, lo:hi], sketch, (((2, 3), (0, 1)), ((), ())),
            preferred_element_type=jnp.float32,
        )
        halves.append(butterfly_sum(part, n_mode, "mode"))
    mapped = jnp.concatenate(halves, axis=1).astype(jnp.bfloat16)

    def local_rows(start, size):
        part = lax.dynamic_slice_in_dim(left_cores, start, size, axis=1)
        out = lax.dot_general(
            part, mapped, (((0, 3), (0, 1)), ((), ())), preferred_element_type=jnp.float32
        )
        return with_layout_constraint(out, Layout(major_to_minor=(0, 1, 2)))

    factor = math.sqrt(R_IN * MODES)
    share = ring_reduce_scatter(local_rows, rows_in, ring)
    flat_share = share.reshape(-1, target)
    gram_part = jnp.dot(flat_share.T, flat_share, precision=HI)
    gram = symmetric_psum(gram_part, len(ring), n_mode)
    basis = orthonormal(flat_share, gram)
    block = basis.reshape(share.shape)
    rounded = block.astype(jnp.bfloat16)
    partial_carry = ring_gather_carries(rounded, left_cores, ring)
    carries = butterfly_sum(partial_carry, n_mode, "mode")
    return (block * factor, carries)


def solution(mesh):
    in_specs = (P("sum", None, "mode", None), P("sum", None, "mode", None), P("mode", None, None))
    out_specs = (P("sum", "mode", None), P("sum", None, None))
    ring = ring_order(mesh)
    return jax.shard_map(
        functools.partial(per_device, ring, mesh.shape["mode"]), mesh=mesh, in_specs=in_specs, out_specs=out_specs, check_vma=False
    )
```

```python
import functools
import math

import jax
import jax.numpy as jnp
from jax import lax
from jax.experimental.layout import Layout, with_layout_constraint
from jax.sharding import PartitionSpec as P

R_IN = 512
MODES = 64
BLOCK = 128

HI = lax.Precision.HIGHEST


def mm(a, b):
    return jnp.dot(a, b, precision=HI, preferred_element_type=jnp.float32)


def tri_inverse(lower):
    n = lower.shape[0]
    h = n // 2
    diag = jnp.stack([lower[:h, :h], lower[h:, h:]])
    eye = jnp.broadcast_to(jnp.eye(h, dtype=jnp.float32), diag.shape)
    inv = lax.linalg.triangular_solve(diag, eye, left_side=True, lower=True)
    corner = -mm(inv[1], mm(lower[h:, :h], inv[0]))
    top = jnp.concatenate([inv[0], jnp.zeros((h, n - h), jnp.float32)], axis=1)
    return jnp.concatenate([top, jnp.concatenate([corner, inv[1]], axis=1)], axis=0)


def orthonormal(sketched, gram, first):
    n = gram.shape[0]
    b = min(BLOCK, n)
    nb = n // b
    eye = jnp.eye(b, dtype=jnp.float32)
    inverses = []
    panels = []
    trailing = gram
    for k in range(nb):
        diag = first if k == 0 else trailing[:b, :b]
        lkk = jnp.linalg.cholesky(diag)
        ikk = tri_inverse(lkk)
        inverses.append(ikk)
        if k < nb - 1:
            panel = mm(trailing[b:, :b], ikk.T)
            panels.append(panel)
            trailing = trailing[b:, b:] - mm(panel, panel.T)
    blocks = []
    for k in range(nb):
        rhs = sketched[:, k * b:(k + 1) * b]
        if k > 0:
            done = jnp.concatenate(blocks, axis=1)
            lrow = jnp.concatenate(
                [panels[j][(k - j - 1) * b:(k - j) * b] for j in range(k)], axis=1
            )
            rhs = rhs - mm(done, lrow.T)
        blocks.append(mm(rhs, inverses[k].T))
    return jnp.concatenate(blocks, axis=1)


def butterfly_sum(x, n, axis="sum"):
    if n & (n - 1):
        return lax.psum(x, axis)
    d = 1
    while d < n:
        x = x + lax.ppermute(x, axis, [(i, i ^ d) for i in range(n)])
        d *= 2
    return x


def symmetric_psum(gram_part, n_sum, n_mode):
    n = gram_part.shape[0]
    b = min(BLOCK, n)
    nb = n // b
    first = gram_part[:b, :b]
    first = butterfly_sum(butterfly_sum(first, n_mode, "mode"), n_sum)
    if nb == 1:
        return first, first
    lower = [(i, j) for i in range(nb) for j in range(i + 1)][1:]
    packed = jnp.stack([gram_part[i * b:(i + 1) * b, j * b:(j + 1) * b] for i, j in lower])
    packed = butterfly_sum(butterfly_sum(packed, n_mode, "mode"), n_sum)
    where = {cell: k for k, cell in enumerate(lower)}

    def cell(i, j):
        if (i, j) == (0, 0):
            return first
        return packed[where[(i, j)]] if j <= i else packed[where[(j, i)]].T

    rows = [jnp.concatenate([cell(i, j) for j in range(nb)], axis=1) for i in range(nb)]
    return jnp.concatenate(rows, axis=0), first


def ring_order(mesh):
    n = mesh.shape["sum"]
    plain = list(range(n))
    try:
        coords = [tuple(int(c) for c in mesh.devices[i, 0].coords) for i in range(n)]
    except (AttributeError, TypeError, IndexError):
        return plain
    axes = [d for d in range(len(coords[0])) if len({c[d] for c in coords}) > 1]
    if len(axes) != 2:
        return plain
    values = [sorted({c[d] for c in coords}) for d in axes]
    if len(values[0]) % 2:
        axes, values = axes[::-1], values[::-1]
    if len(values[0]) % 2 or len(values[0]) * len(values[1]) != n:
        return plain
    where = {(c[axes[0]], c[axes[1]]): i for i, c in enumerate(coords)}
    first, second = values
    cells = [(a, second[0]) for a in first]
    for row, a in enumerate(reversed(first)):
        cols = second[1:] if row % 2 == 0 else second[1:][::-1]
        cells.extend((a, b) for b in cols)
    if len(set(cells)) != n or any(cell not in where for cell in cells):
        return plain
    return [where[cell] for cell in cells]


def ring_reduce_scatter(local, total_rows, ring):
    n = len(ring)
    rows = total_rows // n
    half = rows // 2
    pos = [0] * n
    for p, i in enumerate(ring):
        pos[i] = p
    me = lax.axis_index("sum")
    fwd = [(ring[p], ring[(p + 1) % n]) for p in range(n)]
    bwd = [(ring[p], ring[(p - 1) % n]) for p in range(n)]

    def table(shift, sign):
        return jnp.asarray(
            [[ring[(pos[i] + sign * (shift + t)) % n] for i in range(n)] for t in range(n)],
            dtype=jnp.int32,
        )

    fwd_blocks = table(1, -1)
    bwd_blocks = table(1, 1)

    def piece(block, offset, size):
        start = block * rows + offset
        return local(start, size)

    acc_f = piece(fwd_blocks[0, me], 0, half)
    acc_b = piece(bwd_blocks[0, me], half, rows - half)
    for t in range(1, n):
        acc_f = lax.ppermute(acc_f, "sum", fwd) + piece(fwd_blocks[t, me], 0, half)
        acc_b = lax.ppermute(acc_b, "sum", bwd) + piece(bwd_blocks[t, me], half, rows - half)
    return jnp.concatenate([acc_f, acc_b], axis=0)


def ring_gather_carries(own, left_cores, ring):
    n = len(ring)
    rows = own.shape[0]
    half = rows // 2
    pos = [0] * n
    for p, i in enumerate(ring):
        pos[i] = p
    me = lax.axis_index("sum")
    fwd = [(ring[p], ring[(p + 1) % n]) for p in range(n)]
    bwd = [(ring[p], ring[(p - 1) % n]) for p in range(n)]
    fwd_blocks = jnp.asarray(
        [[ring[(pos[i] - t) % n] for i in range(n)] for t in range(n)], dtype=jnp.int32
    )
    bwd_blocks = jnp.asarray(
        [[ring[(pos[i] + t) % n] for i in range(n)] for t in range(n)], dtype=jnp.int32
    )

    def term(piece, block, offset):
        start = block * rows + offset
        lhs = lax.dynamic_slice_in_dim(left_cores, start, piece.shape[0], axis=1)
        return lax.dot_general(
            piece, lhs, (((0, 1), (1, 2)), ((), ())), preferred_element_type=jnp.float32
        )

    hold_f = own[:half]
    hold_b = own[half:]
    total = term(hold_f, fwd_blocks[0, me], 0) + term(hold_b, bwd_blocks[0, me], half)
    for t in range(1, n):
        hold_f = lax.ppermute(hold_f, "sum", fwd)
        hold_b = lax.ppermute(hold_b, "sum", bwd)
        total = total + term(hold_f, fwd_blocks[t, me], 0)
        total = total + term(hold_b, bwd_blocks[t, me], half)
    return jnp.transpose(total, (1, 0, 2))


def per_device(ring, n_mode, left_cores, right_cores, sketch):
    sum_local, rows_in, mode_local, rank_width = left_cores.shape
    target = sketch.shape[2]
    cut = rank_width // 2
    halves = []
    for lo, hi in ((0, cut), (cut, rank_width)):
        part = lax.dot_general(
            right_cores[:, lo:hi], sketch, (((2, 3), (0, 1)), ((), ())),
            preferred_element_type=jnp.float32,
        )
        halves.append(butterfly_sum(part, n_mode, "mode"))
    mapped = jnp.concatenate(halves, axis=1).astype(jnp.bfloat16)

    def local_rows(start, size):
        part = lax.dynamic_slice_in_dim(left_cores, start, size, axis=1)
        out = lax.dot_general(
            part, mapped, (((0, 3), (0, 1)), ((), ())), preferred_element_type=jnp.float32
        )
        return with_layout_constraint(out, Layout(major_to_minor=(0, 1, 2)))

    factor = math.sqrt(R_IN * MODES)
    share = ring_reduce_scatter(local_rows, rows_in, ring)
    flat_share = share.reshape(-1, target)
    gram_part = jnp.dot(flat_share.T, flat_share, precision=HI)
    gram, first = symmetric_psum(gram_part, len(ring), n_mode)
    basis = orthonormal(flat_share, gram, first)
    block = basis.reshape(share.shape)
    rounded = block.astype(jnp.bfloat16)
    partial_carry = ring_gather_carries(rounded, left_cores, ring)
    carries = butterfly_sum(partial_carry, n_mode, "mode")
    return (block * factor, carries)


def solution(mesh):
    in_specs = (P("sum", None, "mode", None), P("sum", None, "mode", None), P("mode", None, None))
    out_specs = (P("sum", "mode", None), P("sum", None, None))
    ring = ring_order(mesh)
    return jax.shard_map(
        functools.partial(per_device, ring, mesh.shape["mode"]), mesh=mesh, in_specs=in_specs, out_specs=out_specs, check_vma=False
    )
```

```python
import functools
import math

import jax
import jax.numpy as jnp
from jax import lax
from jax.experimental.layout import Layout, with_layout_constraint
from jax.sharding import PartitionSpec as P

R_IN = 512
MODES = 64
BLOCK = 128

HI = lax.Precision.HIGHEST


def mm(a, b):
    return jnp.dot(a, b, precision=HI, preferred_element_type=jnp.float32)


def tri_inverse(lower):
    n = lower.shape[0]
    h = n // 2
    diag = jnp.stack([lower[:h, :h], lower[h:, h:]])
    eye = jnp.broadcast_to(jnp.eye(h, dtype=jnp.float32), diag.shape)
    inv = lax.linalg.triangular_solve(diag, eye, left_side=True, lower=True)
    corner = -mm(inv[1], mm(lower[h:, :h], inv[0]))
    top = jnp.concatenate([inv[0], jnp.zeros((h, n - h), jnp.float32)], axis=1)
    return jnp.concatenate([top, jnp.concatenate([corner, inv[1]], axis=1)], axis=0)


def orthonormal(sketched, blocks_of, nb, b):
    lower = {}
    inverses = []
    for j in range(nb):
        for i in range(j, nb):
            acc = blocks_of[(i, j)]
            if j:
                lhs = jnp.concatenate([lower[(i, k)] for k in range(j)], axis=1)
                rhs = jnp.concatenate([lower[(j, k)] for k in range(j)], axis=1)
                acc = acc - mm(lhs, rhs.T)
            if i == j:
                inverses.append(tri_inverse(jnp.linalg.cholesky(acc)))
            else:
                lower[(i, j)] = mm(acc, inverses[j].T)
    done = []
    for k in range(nb):
        rhs = sketched[:, k * b:(k + 1) * b]
        if k:
            lrow = jnp.concatenate([lower[(k, j)] for j in range(k)], axis=1)
            rhs = rhs - mm(jnp.concatenate(done, axis=1), lrow.T)
        done.append(mm(rhs, inverses[k].T))
    return jnp.concatenate(done, axis=1)


def butterfly_sum(x, n, axis="sum"):
    if n & (n - 1):
        return lax.psum(x, axis)
    d = 1
    while d < n:
        x = x + lax.ppermute(x, axis, [(i, i ^ d) for i in range(n)])
        d *= 2
    return x


def symmetric_psum(gram_part, n_sum, n_mode):
    n = gram_part.shape[0]
    b = min(BLOCK, n)
    nb = n // b
    cells = [(i, j) for i in range(nb) for j in range(i + 1)]
    groups = [cells[:1], cells[1:3], cells[3:]]
    blocks_of = {}
    for group in groups:
        if not group:
            continue
        packed = jnp.stack([gram_part[i * b:(i + 1) * b, j * b:(j + 1) * b] for i, j in group])
        packed = butterfly_sum(butterfly_sum(packed, n_mode, "mode"), n_sum)
        for k, cell in enumerate(group):
            blocks_of[cell] = packed[k]
    return blocks_of, nb, b


def ring_order(mesh):
    n = mesh.shape["sum"]
    plain = list(range(n))
    try:
        coords = [tuple(int(c) for c in mesh.devices[i, 0].coords) for i in range(n)]
    except (AttributeError, TypeError, IndexError):
        return plain
    axes = [d for d in range(len(coords[0])) if len({c[d] for c in coords}) > 1]
    if len(axes) != 2:
        return plain
    values = [sorted({c[d] for c in coords}) for d in axes]
    if len(values[0]) % 2:
        axes, values = axes[::-1], values[::-1]
    if len(values[0]) % 2 or len(values[0]) * len(values[1]) != n:
        return plain
    where = {(c[axes[0]], c[axes[1]]): i for i, c in enumerate(coords)}
    first, second = values
    cells = [(a, second[0]) for a in first]
    for row, a in enumerate(reversed(first)):
        cols = second[1:] if row % 2 == 0 else second[1:][::-1]
        cells.extend((a, b) for b in cols)
    if len(set(cells)) != n or any(cell not in where for cell in cells):
        return plain
    return [where[cell] for cell in cells]


def ring_reduce_scatter(local, total_rows, ring):
    n = len(ring)
    rows = total_rows // n
    half = rows // 2
    pos = [0] * n
    for p, i in enumerate(ring):
        pos[i] = p
    me = lax.axis_index("sum")
    fwd = [(ring[p], ring[(p + 1) % n]) for p in range(n)]
    bwd = [(ring[p], ring[(p - 1) % n]) for p in range(n)]

    def table(shift, sign):
        return jnp.asarray(
            [[ring[(pos[i] + sign * (shift + t)) % n] for i in range(n)] for t in range(n)],
            dtype=jnp.int32,
        )

    fwd_blocks = table(1, -1)
    bwd_blocks = table(1, 1)

    def piece(block, offset, size):
        start = block * rows + offset
        return local(start, size)

    acc_f = piece(fwd_blocks[0, me], 0, half)
    acc_b = piece(bwd_blocks[0, me], half, rows - half)
    for t in range(1, n):
        acc_f = lax.ppermute(acc_f, "sum", fwd) + piece(fwd_blocks[t, me], 0, half)
        acc_b = lax.ppermute(acc_b, "sum", bwd) + piece(bwd_blocks[t, me], half, rows - half)
    return jnp.concatenate([acc_f, acc_b], axis=0)


def ring_gather_carries(own, left_cores, ring):
    n = len(ring)
    rows = own.shape[0]
    half = rows // 2
    pos = [0] * n
    for p, i in enumerate(ring):
        pos[i] = p
    me = lax.axis_index("sum")
    fwd = [(ring[p], ring[(p + 1) % n]) for p in range(n)]
    bwd = [(ring[p], ring[(p - 1) % n]) for p in range(n)]
    fwd_blocks = jnp.asarray(
        [[ring[(pos[i] - t) % n] for i in range(n)] for t in range(n)], dtype=jnp.int32
    )
    bwd_blocks = jnp.asarray(
        [[ring[(pos[i] + t) % n] for i in range(n)] for t in range(n)], dtype=jnp.int32
    )

    def term(piece, block, offset):
        start = block * rows + offset
        lhs = lax.dynamic_slice_in_dim(left_cores, start, piece.shape[0], axis=1)
        return lax.dot_general(
            piece, lhs, (((0, 1), (1, 2)), ((), ())), preferred_element_type=jnp.float32
        )

    hold_f = own[:half]
    hold_b = own[half:]
    total = term(hold_f, fwd_blocks[0, me], 0) + term(hold_b, bwd_blocks[0, me], half)
    for t in range(1, n):
        hold_f = lax.ppermute(hold_f, "sum", fwd)
        hold_b = lax.ppermute(hold_b, "sum", bwd)
        total = total + term(hold_f, fwd_blocks[t, me], 0)
        total = total + term(hold_b, bwd_blocks[t, me], half)
    return jnp.transpose(total, (1, 0, 2))


def per_device(ring, n_mode, left_cores, right_cores, sketch):
    sum_local, rows_in, mode_local, rank_width = left_cores.shape
    target = sketch.shape[2]
    cut = rank_width // 2
    halves = []
    for lo, hi in ((0, cut), (cut, rank_width)):
        part = lax.dot_general(
            right_cores[:, lo:hi], sketch, (((2, 3), (0, 1)), ((), ())),
            preferred_element_type=jnp.float32,
        )
        halves.append(butterfly_sum(part, n_mode, "mode"))
    mapped = jnp.concatenate(halves, axis=1).astype(jnp.bfloat16)

    def local_rows(start, size):
        part = lax.dynamic_slice_in_dim(left_cores, start, size, axis=1)
        out = lax.dot_general(
            part, mapped, (((0, 3), (0, 1)), ((), ())), preferred_element_type=jnp.float32
        )
        return with_layout_constraint(out, Layout(major_to_minor=(0, 1, 2)))

    factor = math.sqrt(R_IN * MODES)
    share = ring_reduce_scatter(local_rows, rows_in, ring)
    flat_share = share.reshape(-1, target)
    gram_part = jnp.dot(flat_share.T, flat_share, precision=HI)
    blocks_of, nb, b = symmetric_psum(gram_part, len(ring), n_mode)
    basis = orthonormal(flat_share, blocks_of, nb, b)
    block = basis.reshape(share.shape)
    rounded = block.astype(jnp.bfloat16)
    partial_carry = ring_gather_carries(rounded, left_cores, ring)
    carries = butterfly_sum(partial_carry, n_mode, "mode")
    return (block * factor, carries)


def solution(mesh):
    in_specs = (P("sum", None, "mode", None), P("sum", None, "mode", None), P("mode", None, None))
    out_specs = (P("sum", "mode", None), P("sum", None, None))
    ring = ring_order(mesh)
    return jax.shard_map(
        functools.partial(per_device, ring, mesh.shape["mode"]), mesh=mesh, in_specs=in_specs, out_specs=out_specs, check_vma=False
    )
```

```python
import functools
import math

import jax
import jax.numpy as jnp
from jax import lax
from jax.experimental.layout import Layout, with_layout_constraint
from jax.sharding import PartitionSpec as P

R_IN = 512
MODES = 64
BLOCK = 128

HI = lax.Precision.HIGHEST


def mm(a, b):
    return jnp.dot(a, b, precision=HI, preferred_element_type=jnp.float32)


def tri_inverse(lower):
    n = lower.shape[0]
    h = n // 2
    diag = jnp.stack([lower[:h, :h], lower[h:, h:]])
    eye = jnp.broadcast_to(jnp.eye(h, dtype=jnp.float32), diag.shape)
    inv = lax.linalg.triangular_solve(diag, eye, left_side=True, lower=True)
    corner = -mm(inv[1], mm(lower[h:, :h], inv[0]))
    top = jnp.concatenate([inv[0], jnp.zeros((h, n - h), jnp.float32)], axis=1)
    return jnp.concatenate([top, jnp.concatenate([corner, inv[1]], axis=1)], axis=0)


def orthonormal(sketched, gram, first):
    n = gram.shape[0]
    b = min(BLOCK, n)
    nb = n // b
    eye = jnp.eye(b, dtype=jnp.float32)
    inverses = []
    panels = []
    trailing = gram
    for k in range(nb):
        diag = first if k == 0 else trailing[:b, :b]
        lkk = jnp.linalg.cholesky(diag)
        ikk = tri_inverse(lkk)
        inverses.append(ikk)
        if k < nb - 1:
            panel = mm(trailing[b:, :b], ikk.T)
            panels.append(panel)
            trailing = trailing[b:, b:] - mm(panel, panel.T)
    blocks = []
    for k in range(nb):
        rhs = sketched[:, k * b:(k + 1) * b]
        if k > 0:
            done = jnp.concatenate(blocks, axis=1)
            lrow = jnp.concatenate(
                [panels[j][(k - j - 1) * b:(k - j) * b] for j in range(k)], axis=1
            )
            rhs = rhs - mm(done, lrow.T)
        blocks.append(mm(rhs, inverses[k].T))
    return jnp.concatenate(blocks, axis=1)


def butterfly_sum(x, n, axis="sum"):
    if n & (n - 1):
        return lax.psum(x, axis)
    d = 1
    while d < n:
        x = x + lax.ppermute(x, axis, [(i, i ^ d) for i in range(n)])
        d *= 2
    return x


def symmetric_psum(gram_part, n_sum, n_mode):
    n = gram_part.shape[0]
    b = min(BLOCK, n)
    nb = n // b
    first = gram_part[:b, :b]
    first = butterfly_sum(butterfly_sum(first, n_mode, "mode"), n_sum)
    if nb == 1:
        return first, first
    lower = [(i, j) for i in range(nb) for j in range(i + 1)][1:]
    packed = jnp.stack([gram_part[i * b:(i + 1) * b, j * b:(j + 1) * b] for i, j in lower])
    packed = butterfly_sum(butterfly_sum(packed, n_mode, "mode"), n_sum)
    where = {cell: k for k, cell in enumerate(lower)}

    def cell(i, j):
        if (i, j) == (0, 0):
            return first
        return packed[where[(i, j)]] if j <= i else packed[where[(j, i)]].T

    rows = [jnp.concatenate([cell(i, j) for j in range(nb)], axis=1) for i in range(nb)]
    return jnp.concatenate(rows, axis=0), first


def ring_order(mesh):
    n = mesh.shape["sum"]
    plain = list(range(n))
    try:
        coords = [tuple(int(c) for c in mesh.devices[i, 0].coords) for i in range(n)]
    except (AttributeError, TypeError, IndexError):
        return plain
    axes = [d for d in range(len(coords[0])) if len({c[d] for c in coords}) > 1]
    if len(axes) != 2:
        return plain
    values = [sorted({c[d] for c in coords}) for d in axes]
    if len(values[0]) % 2:
        axes, values = axes[::-1], values[::-1]
    if len(values[0]) % 2 or len(values[0]) * len(values[1]) != n:
        return plain
    where = {(c[axes[0]], c[axes[1]]): i for i, c in enumerate(coords)}
    first, second = values
    cells = [(a, second[0]) for a in first]
    for row, a in enumerate(reversed(first)):
        cols = second[1:] if row % 2 == 0 else second[1:][::-1]
        cells.extend((a, b) for b in cols)
    if len(set(cells)) != n or any(cell not in where for cell in cells):
        return plain
    return [where[cell] for cell in cells]


def ring_reduce_scatter(local, total_rows, ring):
    n = len(ring)
    rows = total_rows // n
    half = rows // 2
    pos = [0] * n
    for p, i in enumerate(ring):
        pos[i] = p
    me = lax.axis_index("sum")
    fwd = [(ring[p], ring[(p + 1) % n]) for p in range(n)]
    bwd = [(ring[p], ring[(p - 1) % n]) for p in range(n)]

    def table(shift, sign):
        return jnp.asarray(
            [[ring[(pos[i] + sign * (shift + t)) % n] for i in range(n)] for t in range(n)],
            dtype=jnp.int32,
        )

    fwd_blocks = table(1, -1)
    bwd_blocks = table(1, 1)

    def piece(block, offset, size):
        start = block * rows + offset
        return local(start, size)

    acc_f = piece(fwd_blocks[0, me], 0, half)
    acc_b = piece(bwd_blocks[0, me], half, rows - half)
    for t in range(1, n):
        acc_f = lax.ppermute(acc_f, "sum", fwd) + piece(fwd_blocks[t, me], 0, half)
        acc_b = lax.ppermute(acc_b, "sum", bwd) + piece(bwd_blocks[t, me], half, rows - half)
    return jnp.concatenate([acc_f, acc_b], axis=0)


def ring_gather_carries(own, left_cores, ring):
    n = len(ring)
    rows = own.shape[0]
    half = rows // 2
    pos = [0] * n
    for p, i in enumerate(ring):
        pos[i] = p
    me = lax.axis_index("sum")
    fwd = [(ring[p], ring[(p + 1) % n]) for p in range(n)]
    bwd = [(ring[p], ring[(p - 1) % n]) for p in range(n)]
    fwd_blocks = jnp.asarray(
        [[ring[(pos[i] - t) % n] for i in range(n)] for t in range(n)], dtype=jnp.int32
    )
    bwd_blocks = jnp.asarray(
        [[ring[(pos[i] + t) % n] for i in range(n)] for t in range(n)], dtype=jnp.int32
    )

    def term(piece, block, offset):
        start = block * rows + offset
        lhs = lax.dynamic_slice_in_dim(left_cores, start, piece.shape[0], axis=1)
        return lax.dot_general(
            piece, lhs, (((0, 1), (1, 2)), ((), ())), preferred_element_type=jnp.float32
        )

    hold_f = own[:half]
    hold_b = own[half:]
    total = term(hold_f, fwd_blocks[0, me], 0) + term(hold_b, bwd_blocks[0, me], half)
    for t in range(1, n):
        hold_f = lax.ppermute(hold_f, "sum", fwd)
        hold_b = lax.ppermute(hold_b, "sum", bwd)
        total = total + term(hold_f, fwd_blocks[t, me], 0)
        total = total + term(hold_b, bwd_blocks[t, me], half)
    return jnp.transpose(total, (1, 0, 2))


def per_device(ring, n_mode, left_cores, right_cores, sketch):
    sum_local, rows_in, mode_local, rank_width = left_cores.shape
    target = sketch.shape[2]
    pieces = 4 if rank_width % 64 == 0 else 1
    step = rank_width // pieces
    halves = []
    for lo, hi in [(p * step, (p + 1) * step) for p in range(pieces)]:
        part = lax.dot_general(
            right_cores[:, lo:hi], sketch, (((2, 3), (0, 1)), ((), ())),
            preferred_element_type=jnp.float32,
        )
        halves.append(butterfly_sum(part, n_mode, "mode"))
    mapped = jnp.concatenate(halves, axis=1).astype(jnp.bfloat16)

    def local_rows(start, size):
        part = lax.dynamic_slice_in_dim(left_cores, start, size, axis=1)
        out = lax.dot_general(
            part, mapped, (((0, 3), (0, 1)), ((), ())), preferred_element_type=jnp.float32
        )
        return with_layout_constraint(out, Layout(major_to_minor=(0, 1, 2)))

    factor = math.sqrt(R_IN * MODES)
    share = ring_reduce_scatter(local_rows, rows_in, ring)
    flat_share = share.reshape(-1, target)
    gram_part = jnp.dot(flat_share.T, flat_share, precision=HI)
    gram, first = symmetric_psum(gram_part, len(ring), n_mode)
    basis = orthonormal(flat_share, gram, first)
    block = basis.reshape(share.shape)
    rounded = block.astype(jnp.bfloat16)
    partial_carry = ring_gather_carries(rounded, left_cores, ring)
    carries = butterfly_sum(partial_carry, n_mode, "mode")
    return (block * factor, carries)


def solution(mesh):
    in_specs = (P("sum", None, "mode", None), P("sum", None, "mode", None), P("mode", None, None))
    out_specs = (P("sum", "mode", None), P("sum", None, None))
    ring = ring_order(mesh)
    return jax.shard_map(
        functools.partial(per_device, ring, mesh.shape["mode"]), mesh=mesh, in_specs=in_specs, out_specs=out_specs, check_vma=False
    )
```
